128 devices in a mesh: dp: 32 (over x, y, core), tensor: 4 (over z).
Axes of the slice: x: 4, y: 4, z: 4, core: 2. Of those that a mesh axis runs over, the one named last changes fastest.
Arguments:
- query: bfloat16 [32768, 5120], P('dp', 'tensor'), may hold values from -6 to 6
- keys: bfloat16 [32768, 1024], P('dp', 'tensor'), may hold values from -6 to 6
- values: bfloat16 [32768, 1024], P('dp', 'tensor'), may hold values from -6 to 6
- out_weight: bfloat16 [5120, 2560], P('tensor', 'dp'), may hold values from -0.078125 to 0.078125
- loss_grad: bfloat16 [32768, 2560], P('dp', 'tensor'), may hold values from -6 to 6
- lengths: int32 [32, 16], P('dp'), may hold values from 1 to 512, 1024 in all within a row
- languages: int32 [32, 16], P('dp'), may hold values from 0 to 28
- labels: int32 [32768], P('dp'), may hold values from -100 to 152063, as said below
Outputs:
- attention_result: bfloat16 [32768, 5120], P('dp', 'tensor')
- query_gradient: bfloat16 [32768, 5120], P('dp', 'tensor')
- key_gradient: bfloat16 [32768, 1024], P('dp', 'tensor')
- value_gradient: bfloat16 [32768, 1024], P('dp', 'tensor')
- projection_gradient: bfloat16 [5120, 2560], P('tensor')
The draws below stay inside these ranges and needn't reach their ends.
Inputs may be any that keep to these rules, and one draw needn't show every extreme that they name: `labels`: each label is -100, meaning no loss on that token, or a token id below 152064.
All inputs are finite; a program needn't handle non-finite values.
Results may differ from the reference program's by a relative error of at most 0.02.
Values may be sent and summed in bfloat16 or wider, within the bound.
No kernel may reach another device: no remote copies, remote signals or barrier semaphores. Data moves between devices by JAX's collectives and lax.ppermute only.
A program may use at most 192 MiB of HBM per device.

```python
import math
import jax
import jax.numpy as jnp
import numpy as np
from jax import lax

QUERY_HEADS = 40
KEY_VALUE_HEADS = 8
HEAD_SIZE = 128
VOCAB = 152064
DWIN = 2560
LANGS = 29
DOCS = 16
PACK_TOKENS = 1024
TOTAL_TOKENS = 32768
N_DP = 32


def base_sample(key, shape):
    return jnp.clip(jax.random.normal(key, shape), -5.0, 5.0)


def draw_query(key, part):
    base_value = base_sample(jax.random.fold_in(key, 1), (TOTAL_TOKENS, QUERY_HEADS * HEAD_SIZE))
    return base_value.astype(jnp.bfloat16)


def draw_keys(key, part):
    base_value = base_sample(jax.random.fold_in(key, 2), (TOTAL_TOKENS, KEY_VALUE_HEADS * HEAD_SIZE))
    return base_value.astype(jnp.bfloat16)


def draw_labels(key, part):
    rolls = jax.random.randint(jax.random.fold_in(key, 1), (TOTAL_TOKENS,), 0, 10)
    token_ids = jax.random.randint(jax.random.fold_in(key, 2), (TOTAL_TOKENS,), 0, VOCAB)
    places = jnp.arange(TOTAL_TOKENS, dtype=jnp.int32)
    last_row = places == TOTAL_TOKENS - 1
    token_ids = jnp.where(last_row, VOCAB - 1, token_ids)
    return jnp.where((rolls < 3) & jnp.logical_not(last_row), -100, token_ids).astype(jnp.int32)


def set_ends(array, rng, low, largest):
    dims = array.shape
    index_at = [jax.random.randint(jax.random.fold_in(rng, axis), (), 0, dims[axis]) for axis in range(len(dims))]
    array = array.at[tuple(index_at)].set(low)
    longest = dims.index(max(dims))
    index_at[longest] = (index_at[longest] + 1) % dims[longest]
    return array.at[tuple(index_at)].set(largest)


def steps_of(stream_key, dims, split, low, high):
    loudness = 1.0
    for dim, blocks in split:
        steps = jax.random.uniform(jax.random.fold_in(jax.random.fold_in(stream_key, 6), dim), (blocks,), jnp.float32, low / len(split), high / len(split))
        loudness = loudness * jnp.repeat(jnp.exp(steps), dims[dim] // blocks).reshape((-1,) + (1,) * (len(dims) - 1 - dim))
    return loudness


def cumulative_ranks(amount, skew):
    portions = [(1 << 20) // math.isqrt(grade ** skew) + 1 for grade in range(1, amount + 1)]
    deviation = 1 + sum(portions) // (1 << 30)
    return np.cumsum(np.array([max(1, weight // deviation) for weight in portions]))


def skewed_ids(stream_key, dims, amount, lean):
    table = cumulative_ranks(amount, lean)
    pick = jax.random.randint(jax.random.fold_in(stream_key, 1), dims, 0, int(table[amount - 1]))
    rank = jnp.searchsorted(jnp.asarray(table, jnp.int32), pick, side="right")
    return jax.random.permutation(jax.random.fold_in(stream_key, 2), amount)[rank].astype(jnp.int32)


def split_up(number_of, total, most, lean):
    loads = [(1 << 20) // math.isqrt(standing ** lean) + 1 for standing in range(2, number_of + 1)]
    rest, given = total - most - (number_of - 1), [1] * (number_of - 1)
    while rest > 0:
        movable = [i for i in range(number_of - 1) if given[i] < most]
        whole, left = sum([loads[i] for i in movable]), rest
        for i in movable:
            more = min(most - given[i], max(1, left * loads[i] // whole), rest)
            given[i] = given[i] + more
            rest = rest - more
    return np.array([most] + given)


def ragged_sizes(rng, count, total, most, slope):
    if count == 2:
        one = jax.random.randint(rng, (), max(1, total - most), min(most, total - 1) + 1)
        return jnp.stack([one, total - one])
    sizes = jnp.asarray(split_up(count, total, most, slope), jnp.int32)
    couples = (count - 1) // 2
    donor, receiver = sizes[1:1 + 2 * couples:2], sizes[2:2 + 2 * couples:2]
    margin = jnp.minimum(donor - 1, most - receiver)
    moved = jax.random.randint(jax.random.fold_in(rng, 1), (couples,), 0, 1 << 20) % (margin + 1)
    sizes = sizes.at[1:1 + 2 * couples:2].set(donor - moved).at[2:2 + 2 * couples:2].set(receiver + moved)
    return sizes[jax.random.permutation(jax.random.fold_in(rng, 2), count)]


def scatter_about(rng, shape, scale, bound, shards=(), kind=jnp.bfloat16):
    values = jax.random.normal(rng, shape, jnp.float32) * scale
    if len(shards) > 0:
        values = steps_of(rng, shape, shards, -0.22, 0.18) * values
    return jnp.clip(values, min=-bound, max=bound).astype(kind)


def setup_inputs(seed: int = 0) -> dict:
    key_of = jax.random.split(jax.random.key(seed), 9)
    query = draw_query(jax.random.fold_in(key_of[8], 71), 0)
    keys = draw_keys(jax.random.fold_in(key_of[8], 71), 0)
    values = scatter_about(key_of[2], (TOTAL_TOKENS, KEY_VALUE_HEADS * HEAD_SIZE), 1.0, 6.0, ((0, 32), (1, 4)))
    out_weight = scatter_about(key_of[3], (QUERY_HEADS * HEAD_SIZE, DWIN), (QUERY_HEADS * HEAD_SIZE) ** -0.5, 0.078125, ((0, 4), (1, 32)))
    loss_grad = scatter_about(key_of[4], (TOTAL_TOKENS, DWIN), 1.0, 6.0, ((0, 32), (1, 4)))
    lengths = jax.vmap(lambda own: ragged_sizes(own, DOCS, PACK_TOKENS, PACK_TOKENS // 2, 2))(jax.random.split(key_of[5], N_DP)).reshape((N_DP, DOCS)).astype(jnp.int32)
    languages = set_ends(skewed_ids(key_of[6], (N_DP, DOCS), LANGS, 2), jax.random.fold_in(key_of[6], 3), 0, LANGS - 1).astype(jnp.int32)
    labels = draw_labels(jax.random.fold_in(key_of[8], 71), 0)
    return {"query": query, "keys": keys, "values": values, "out_weight": out_weight, "loss_grad": loss_grad, "lengths": lengths, "languages": languages, "labels": labels}


def token_docs(length_row, row_count):
    doc_ends = jnp.cumsum(length_row).astype(jnp.int32)
    places = jnp.arange(row_count, dtype=jnp.int32)
    return lax.optimization_barrier(jnp.sum((places[:, None] >= doc_ends[None, :]).astype(jnp.int32), axis=1))

def masked_scores(query_rows, key_rows, allowed, factor):
    scores = jnp.einsum('rgd,kd->grk', query_rows.astype(jnp.float32), key_rows.astype(jnp.float32)) * factor
    return jnp.where(allowed[None], scores, -1e+30)

def forward_group(query_rows, key_rows, value_rows, allowed, factor):
    scores = masked_scores(query_rows, key_rows, allowed, factor)
    row_top = lax.optimization_barrier(jnp.max(scores, axis=2, keepdims=True))
    log_total = row_top + jnp.log(lax.optimization_barrier(jnp.sum(jnp.exp(scores - row_top), axis=2, keepdims=True)))
    weights = jnp.exp(scores - log_total).astype(jnp.bfloat16)
    result = jnp.einsum('grk,kd->rgd', weights.astype(jnp.float32), value_rows.astype(jnp.float32))
    return (result.astype(jnp.bfloat16), log_total[:, :, 0])

def backward_group(query_rows, key_rows, value_rows, allowed, out_rows, log_rows, grad_rows, factor):
    scores = masked_scores(query_rows, key_rows, allowed, factor)
    weights = jnp.exp(scores - log_rows[:, :, None])
    grad_wide = grad_rows.astype(jnp.float32)
    value_gradient = jnp.einsum('grk,rgd->kd', weights.astype(jnp.bfloat16).astype(jnp.float32), grad_wide)
    weight_grad = jnp.einsum('rgd,kd->grk', grad_wide, value_rows.astype(jnp.float32))
    diagonal_term = jnp.einsum('rgd,rgd->gr', grad_wide, out_rows.astype(jnp.float32))
    score_grad = (weights * (weight_grad - diagonal_term[:, :, None]) * factor).astype(jnp.bfloat16)
    score_wide = score_grad.astype(jnp.float32)
    query_gradient = jnp.einsum('grk,kd->rgd', score_wide, key_rows.astype(jnp.float32))
    key_gradient = jnp.einsum('grk,rgd->kd', score_wide, query_rows.astype(jnp.float32))
    return (query_gradient, key_gradient, value_gradient)

def reference(query, keys, values, out_weight, loss_grad, lengths, languages, labels):
    factor = 1.0 / math.sqrt(HEAD_SIZE)
    group_size = QUERY_HEADS // KEY_VALUE_HEADS
    places = jnp.arange(PACK_TOKENS, dtype=jnp.int32)

    def layout(length_row):
        doc_ids = token_docs(length_row, PACK_TOKENS)
        return (doc_ids[:, None] == doc_ids[None, :]) & (places[:, None] >= places[None, :])

    def pack_forward(item):
        packed_query, key_pack, value_pack, length_row = item
        allowed = layout(length_row)
        query_by_head = packed_query.reshape(PACK_TOKENS, KEY_VALUE_HEADS, group_size, HEAD_SIZE)
        outs = []
        logs = []
        for head_cluster in range(KEY_VALUE_HEADS):
            result, log_rows = forward_group(query_by_head[:, head_cluster], key_pack[:, head_cluster * HEAD_SIZE:(head_cluster + 1) * HEAD_SIZE], value_pack[:, head_cluster * HEAD_SIZE:(head_cluster + 1) * HEAD_SIZE], allowed, factor)
            outs.append(result.reshape(PACK_TOKENS, group_size * HEAD_SIZE))
            logs.append(log_rows)
        return (jnp.concatenate(outs, axis=1), jnp.stack(logs, axis=0))
    query_packs = query.reshape(N_DP, PACK_TOKENS, QUERY_HEADS * HEAD_SIZE)
    packed_keys = keys.reshape(N_DP, PACK_TOKENS, KEY_VALUE_HEADS * HEAD_SIZE)
    packed_values = values.reshape(N_DP, PACK_TOKENS, KEY_VALUE_HEADS * HEAD_SIZE)
    attn_packs, log_packs = lax.map(pack_forward, (query_packs, packed_keys, packed_values, lengths))
    attention_result = attn_packs.reshape(TOTAL_TOKENS, QUERY_HEADS * HEAD_SIZE)
    doc_all = jax.vmap(lambda row: token_docs(row, PACK_TOKENS))(lengths)
    token_lang = jnp.take_along_axis(languages, doc_all, axis=1).reshape(TOTAL_TOKENS)
    counted = labels != -100
    hits = ((token_lang[:, None] == jnp.arange(LANGS, dtype=jnp.int32)[None, :]) & counted[:, None]).astype(jnp.int32)
    counts = lax.optimization_barrier(jnp.sum(hits, axis=0)).astype(jnp.float32)
    lang_weight = jnp.sqrt(jnp.sum(counts) / (LANGS * jnp.maximum(counts, 1.0)))
    token_weight = jnp.where(counted, lang_weight[token_lang], 0.0)
    weighted = (token_weight[:, None] * loss_grad.astype(jnp.float32)).astype(jnp.bfloat16)
    out_grad = jnp.dot(weighted, out_weight.T, preferred_element_type=jnp.float32).astype(jnp.bfloat16)
    projection_gradient = jnp.dot(attention_result.T, weighted, preferred_element_type=jnp.float32).astype(jnp.bfloat16)

    def pack_backward(item):
        packed_query, key_pack, value_pack, length_row, attention_per_pack, log_pack, gradient_per_pack = item
        allowed = layout(length_row)
        query_by_head = packed_query.reshape(PACK_TOKENS, KEY_VALUE_HEADS, group_size, HEAD_SIZE)
        attention_by_head = attention_per_pack.reshape(PACK_TOKENS, KEY_VALUE_HEADS, group_size, HEAD_SIZE)
        gradient_by_head = gradient_per_pack.reshape(PACK_TOKENS, KEY_VALUE_HEADS, group_size, HEAD_SIZE)
        query_parts = []
        key_parts = []
        value_parts = []
        for head_cluster in range(KEY_VALUE_HEADS):
            query_part, key_part, value_part = backward_group(query_by_head[:, head_cluster], key_pack[:, head_cluster * HEAD_SIZE:(head_cluster + 1) * HEAD_SIZE], value_pack[:, head_cluster * HEAD_SIZE:(head_cluster + 1) * HEAD_SIZE], allowed, attention_by_head[:, head_cluster], log_pack[head_cluster], gradient_by_head[:, head_cluster], factor)
            query_parts.append(query_part.astype(jnp.bfloat16).reshape(PACK_TOKENS, group_size * HEAD_SIZE))
            key_parts.append(key_part.astype(jnp.bfloat16))
            value_parts.append(value_part.astype(jnp.bfloat16))
        return (jnp.concatenate(query_parts, axis=1), jnp.concatenate(key_parts, axis=1), jnp.concatenate(value_parts, axis=1))
    query_gradient, key_gradient, value_gradient = lax.map(pack_backward, (query_packs, packed_keys, packed_values, lengths, attn_packs, log_packs, out_grad.reshape(N_DP, PACK_TOKENS, QUERY_HEADS * HEAD_SIZE)))
    return (attention_result, query_gradient.reshape(TOTAL_TOKENS, QUERY_HEADS * HEAD_SIZE), key_gradient.reshape(TOTAL_TOKENS, KEY_VALUE_HEADS * HEAD_SIZE), value_gradient.reshape(TOTAL_TOKENS, KEY_VALUE_HEADS * HEAD_SIZE), projection_gradient)
```

```python
import math

import jax
import jax.numpy as jnp
from jax import lax
from jax.sharding import PartitionSpec as P

QUERY_HEADS = 40
KEY_VALUE_HEADS = 8
HEAD_SIZE = 128
LANGS = 29
DOCS = 16


def token_docs(length_row, row_count):
    doc_ends = jnp.cumsum(length_row)
    places = jnp.arange(row_count, dtype=jnp.int32)
    return jnp.sum((places[:, None] >= doc_ends[None, :]).astype(jnp.int32), axis=1)


def masked_scores(query_rows, key_rows, allowed, factor):
    scores = (
        jnp.einsum("rgd,kd->grk", query_rows, key_rows, preferred_element_type=jnp.float32) * factor
    )
    return jnp.where(allowed[None], scores, -1e30)


def block_forward(query_rows, key_rows, value_rows, allowed, factor):
    scores = masked_scores(query_rows, key_rows, allowed, factor)
    row_top = jnp.max(scores, axis=2, keepdims=True)
    log_total = row_top + jnp.log(jnp.sum(jnp.exp(scores - row_top), axis=2, keepdims=True))
    weights = jnp.exp(scores - log_total).astype(jnp.bfloat16)
    result = jnp.einsum("grk,kd->rgd", weights, value_rows, preferred_element_type=jnp.float32)
    return (result.astype(jnp.bfloat16), log_total[:, :, 0])


def block_backward(
    query_rows, key_rows, value_rows, allowed, out_rows, log_rows, grad_rows, factor
):
    scores = masked_scores(query_rows, key_rows, allowed, factor)
    weights = jnp.exp(scores - log_rows[:, :, None])
    value_gradient = jnp.einsum(
        "grk,rgd->kd", weights.astype(jnp.bfloat16), grad_rows, preferred_element_type=jnp.float32
    )
    weight_grad = jnp.einsum(
        "rgd,kd->grk", grad_rows, value_rows, preferred_element_type=jnp.float32
    )
    diagonal_term = jnp.einsum(
        "rgd,rgd->gr", grad_rows, out_rows, preferred_element_type=jnp.float32
    )
    score_grad = (weights * (weight_grad - diagonal_term[:, :, None]) * factor).astype(jnp.bfloat16)
    query_gradient = jnp.einsum(
        "grk,kd->rgd", score_grad, key_rows, preferred_element_type=jnp.float32
    )
    key_gradient = jnp.einsum(
        "grk,rgd->kd", score_grad, query_rows, preferred_element_type=jnp.float32
    )
    return (query_gradient, key_gradient, value_gradient)


def pack_layout(doc_ids):
    row_count = doc_ids.shape[0]
    places = jnp.arange(row_count, dtype=jnp.int32)
    allowed = (doc_ids[:, None] == doc_ids[None, :]) & (places[:, None] >= places[None, :])
    half_rows = row_count // 2
    key_step = row_count // 8
    first_row = jnp.min(jnp.where(doc_ids == doc_ids[half_rows], places, row_count))
    return (allowed, half_rows, key_step, first_row // key_step)


def pack_forward(query, keys, values, doc_ids, factor):
    allowed, half_rows, key_step, bucket = pack_layout(doc_ids)
    row_count = doc_ids.shape[0]
    group_size = QUERY_HEADS // KEY_VALUE_HEADS
    outs = []
    logs = []
    for head_cluster in range(keys.shape[1] // HEAD_SIZE):
        query_part = query[
            :, head_cluster * group_size * HEAD_SIZE : (head_cluster + 1) * group_size * HEAD_SIZE
        ].reshape(row_count, group_size, HEAD_SIZE)
        key_part = keys[:, head_cluster * HEAD_SIZE : (head_cluster + 1) * HEAD_SIZE]
        value_part = values[:, head_cluster * HEAD_SIZE : (head_cluster + 1) * HEAD_SIZE]
        early_out, early_log = block_forward(
            query_part[:half_rows],
            key_part[:half_rows],
            value_part[:half_rows],
            allowed[:half_rows, :half_rows],
            factor,
        )

        def later_block(bucket_id):
            first_key = bucket_id * key_step

            def run_block(operands):
                query_late, key_all, value_all = operands
                return block_forward(
                    query_late,
                    key_all[first_key:],
                    value_all[first_key:],
                    allowed[half_rows:, first_key:],
                    factor,
                )

            return run_block

        late_out, late_log = lax.switch(
            bucket,
            [later_block(bucket_id) for bucket_id in range(5)],
            (query_part[half_rows:], key_part, value_part),
        )
        outs.append(
            jnp.concatenate([early_out, late_out], axis=0).reshape(
                row_count, group_size * HEAD_SIZE
            )
        )
        logs.append(jnp.concatenate([early_log, late_log], axis=1))
    return (jnp.concatenate(outs, axis=1), jnp.stack(logs, axis=0))


def pack_backward(query, keys, values, doc_ids, attn_rows, log_rows, grad_rows, factor):
    allowed, half_rows, key_step, bucket = pack_layout(doc_ids)
    row_count = doc_ids.shape[0]
    group_size = QUERY_HEADS // KEY_VALUE_HEADS
    query_parts = []
    key_parts = []
    value_parts = []
    for head_cluster in range(keys.shape[1] // HEAD_SIZE):
        span = slice(
            head_cluster * group_size * HEAD_SIZE, (head_cluster + 1) * group_size * HEAD_SIZE
        )
        query_part = query[:, span].reshape(row_count, group_size, HEAD_SIZE)
        attn_part = attn_rows[:, span].reshape(row_count, group_size, HEAD_SIZE)
        grad_part = grad_rows[:, span].reshape(row_count, group_size, HEAD_SIZE)
        key_part = keys[:, head_cluster * HEAD_SIZE : (head_cluster + 1) * HEAD_SIZE]
        value_part = values[:, head_cluster * HEAD_SIZE : (head_cluster + 1) * HEAD_SIZE]
        log_part = log_rows[head_cluster]
        early_query, early_key, early_value = block_backward(
            query_part[:half_rows],
            key_part[:half_rows],
            value_part[:half_rows],
            allowed[:half_rows, :half_rows],
            attn_part[:half_rows],
            log_part[:, :half_rows],
            grad_part[:half_rows],
            factor,
        )

        def later_block(bucket_id):
            first_key = bucket_id * key_step

            def run_block(operands):
                query_late, key_all, value_all, attn_late, log_late, grad_late = operands
                late_query, late_key, late_value = block_backward(
                    query_late,
                    key_all[first_key:],
                    value_all[first_key:],
                    allowed[half_rows:, first_key:],
                    attn_late,
                    log_late,
                    grad_late,
                    factor,
                )
                return (
                    late_query,
                    jnp.pad(late_key, ((first_key, 0), (0, 0))),
                    jnp.pad(late_value, ((first_key, 0), (0, 0))),
                )

            return run_block

        late_query, late_key, late_value = lax.switch(
            bucket,
            [later_block(bucket_id) for bucket_id in range(5)],
            (
                query_part[half_rows:],
                key_part,
                value_part,
                attn_part[half_rows:],
                log_part[:, half_rows:],
                grad_part[half_rows:],
            ),
        )
        tail_rows = row_count - half_rows
        key_total = late_key + jnp.pad(early_key, ((0, tail_rows), (0, 0)))
        value_total = late_value + jnp.pad(early_value, ((0, tail_rows), (0, 0)))
        query_parts.append(
            jnp.concatenate([early_query, late_query], axis=0)
            .astype(jnp.bfloat16)
            .reshape(row_count, group_size * HEAD_SIZE)
        )
        key_parts.append(key_total.astype(jnp.bfloat16))
        value_parts.append(value_total.astype(jnp.bfloat16))
    return (
        jnp.concatenate(query_parts, axis=1),
        jnp.concatenate(key_parts, axis=1),
        jnp.concatenate(value_parts, axis=1),
    )


def shards(query, keys, values, out_weight, loss_grad, lengths, languages, labels):
    factor = 1.0 / math.sqrt(HEAD_SIZE)
    row_count = query.shape[0]
    doc_ids = token_docs(lengths[0], row_count)
    attention_result, log_rows = pack_forward(query, keys, values, doc_ids, factor)
    token_lang = jnp.sum(
        jnp.where(
            doc_ids[:, None] == jnp.arange(DOCS, dtype=jnp.int32)[None, :], languages[0][None, :], 0
        ),
        axis=1,
    )
    counted = labels != -100
    lang_match = token_lang[:, None] == jnp.arange(LANGS, dtype=jnp.int32)[None, :]
    local_counts = jnp.sum((lang_match & counted[:, None]).astype(jnp.int32), axis=0)
    counts = jnp.sum(lax.all_gather(local_counts, "dp"), axis=0).astype(jnp.float32)
    lang_weight = jnp.sqrt(jnp.sum(counts) / (LANGS * jnp.maximum(counts, 1.0)))
    token_weight = jnp.where(
        counted, jnp.sum(jnp.where(lang_match, lang_weight[None, :], 0.0), axis=1), 0.0
    )
    full_grad = lax.all_gather(loss_grad, "tensor", axis=1, tiled=True)
    weighted = (token_weight[:, None] * full_grad.astype(jnp.float32)).astype(jnp.bfloat16)
    out_grad = lax.dot_general(
        weighted,
        lax.all_gather(out_weight, "dp", axis=1, tiled=True),
        (((1,), (1,)), ((), ())),
        preferred_element_type=jnp.float32,
    ).astype(jnp.bfloat16)
    local_term = lax.dot_general(
        attention_result, weighted, (((0,), (0,)), ((), ())), preferred_element_type=jnp.float32
    )
    projection_part = lax.psum_scatter(local_term, "dp", scatter_dimension=0, tiled=True)
    projection_gradient = lax.all_gather(
        projection_part.astype(jnp.bfloat16), "dp", axis=0, tiled=True
    )
    query_gradient, key_gradient, value_gradient = pack_backward(
        query, keys, values, doc_ids, attention_result, log_rows, out_grad, factor
    )
    return (attention_result, query_gradient, key_gradient, value_gradient, projection_gradient)


def solution(mesh):
    in_specs = (
        P("dp", "tensor"),
        P("dp", "tensor"),
        P("dp", "tensor"),
        P("tensor", "dp"),
        P("dp", "tensor"),
        P("dp", None),
        P("dp", None),
        P("dp"),
    )
    out_specs = (
        P("dp", "tensor"),
        P("dp", "tensor"),
        P("dp", "tensor"),
        P("dp", "tensor"),
        P("tensor", None),
    )
    return jax.shard_map(shards, mesh=mesh, in_specs=in_specs, out_specs=out_specs, check_vma=False)
```

```python
import math

import jax
import jax.numpy as jnp
from jax import lax
from jax.sharding import PartitionSpec as P


QUERY_HEADS = 40
KEY_VALUE_HEADS = 8
HEAD_SIZE = 128
LANGS = 29
DOCS = 16


def token_docs(length_row, row_count):
    doc_ends = jnp.cumsum(length_row)
    places = jnp.arange(row_count, dtype=jnp.int32)
    return jnp.sum((places[:, None] >= doc_ends[None, :]).astype(jnp.int32), axis=1)


def masked_scores(query_rows, key_rows, allowed, factor):
    scores = (
        jnp.einsum("rgd,kd->grk", query_rows, key_rows, preferred_element_type=jnp.float32) * factor
    )
    return jnp.where(allowed[None], scores, -1e30)


def block_forward(query_rows, key_rows, value_rows, allowed, factor):
    scores = masked_scores(query_rows, key_rows, allowed, factor)
    row_top = jnp.max(scores, axis=2, keepdims=True)
    log_total = row_top + jnp.log(jnp.sum(jnp.exp(scores - row_top), axis=2, keepdims=True))
    weights = jnp.exp(scores - log_total).astype(jnp.bfloat16)
    result = jnp.einsum("grk,kd->rgd", weights, value_rows, preferred_element_type=jnp.float32)
    return (result.astype(jnp.bfloat16), log_total[:, :, 0])


def block_backward(
    query_rows, key_rows, value_rows, allowed, out_rows, log_rows, grad_rows, factor
):
    scores = masked_scores(query_rows, key_rows, allowed, factor)
    weights = jnp.exp(scores - log_rows[:, :, None])
    value_gradient = jnp.einsum(
        "grk,rgd->kd", weights.astype(jnp.bfloat16), grad_rows, preferred_element_type=jnp.float32
    )
    weight_grad = jnp.einsum(
        "rgd,kd->grk", grad_rows, value_rows, preferred_element_type=jnp.float32
    )
    diagonal_term = jnp.einsum(
        "rgd,rgd->gr", grad_rows, out_rows, preferred_element_type=jnp.float32
    )
    score_grad = (weights * (weight_grad - diagonal_term[:, :, None]) * factor).astype(jnp.bfloat16)
    query_gradient = jnp.einsum(
        "grk,kd->rgd", score_grad, key_rows, preferred_element_type=jnp.float32
    )
    key_gradient = jnp.einsum(
        "grk,rgd->kd", score_grad, query_rows, preferred_element_type=jnp.float32
    )
    return (query_gradient, key_gradient, value_gradient)


def pack_layout(doc_ids):
    row_count = doc_ids.shape[0]
    places = jnp.arange(row_count, dtype=jnp.int32)
    allowed = (doc_ids[:, None] == doc_ids[None, :]) & (places[:, None] >= places[None, :])
    half_rows = row_count // 2
    key_step = row_count // 8
    first_row = jnp.min(jnp.where(doc_ids == doc_ids[half_rows], places, row_count))
    return (allowed, half_rows, key_step, first_row // key_step)


def pack_forward(query, keys, values, doc_ids, factor):
    allowed, half_rows, key_step, bucket = pack_layout(doc_ids)
    row_count = doc_ids.shape[0]
    group_size = QUERY_HEADS // KEY_VALUE_HEADS
    outs = []
    logs = []
    for head_cluster in range(keys.shape[1] // HEAD_SIZE):
        query_part = query[
            :, head_cluster * group_size * HEAD_SIZE : (head_cluster + 1) * group_size * HEAD_SIZE
        ].reshape(row_count, group_size, HEAD_SIZE)
        key_part = keys[:, head_cluster * HEAD_SIZE : (head_cluster + 1) * HEAD_SIZE]
        value_part = values[:, head_cluster * HEAD_SIZE : (head_cluster + 1) * HEAD_SIZE]
        early_out, early_log = block_forward(
            query_part[:half_rows],
            key_part[:half_rows],
            value_part[:half_rows],
            allowed[:half_rows, :half_rows],
            factor,
        )

        def later_block(bucket_id):
            first_key = bucket_id * key_step

            def run_block(operands):
                query_late, key_all, value_all = operands
                return block_forward(
                    query_late,
                    key_all[first_key:],
                    value_all[first_key:],
                    allowed[half_rows:, first_key:],
                    factor,
                )

            return run_block

        late_out, late_log = lax.switch(
            bucket,
            [later_block(bucket_id) for bucket_id in range(5)],
            (query_part[half_rows:], key_part, value_part),
        )
        outs.append(
            jnp.concatenate([early_out, late_out], axis=0).reshape(
                row_count, group_size * HEAD_SIZE
            )
        )
        logs.append(jnp.concatenate([early_log, late_log], axis=1))
    return (jnp.concatenate(outs, axis=1), jnp.stack(logs, axis=0))


def cluster_backward(
    head_cluster, query, keys, values, layout, attn_rows, log_rows, grad_rows, factor
):
    allowed, half_rows, key_step, bucket = layout
    row_count = query.shape[0]
    group_size = QUERY_HEADS // KEY_VALUE_HEADS
    span = slice(
        head_cluster * group_size * HEAD_SIZE, (head_cluster + 1) * group_size * HEAD_SIZE
    )
    query_part = query[:, span].reshape(row_count, group_size, HEAD_SIZE)
    attn_part = attn_rows[:, span].reshape(row_count, group_size, HEAD_SIZE)
    grad_part = grad_rows[:, span].reshape(row_count, group_size, HEAD_SIZE)
    key_part = keys[:, head_cluster * HEAD_SIZE : (head_cluster + 1) * HEAD_SIZE]
    value_part = values[:, head_cluster * HEAD_SIZE : (head_cluster + 1) * HEAD_SIZE]
    log_part = log_rows[head_cluster]
    early_query, early_key, early_value = block_backward(
        query_part[:half_rows],
        key_part[:half_rows],
        value_part[:half_rows],
        allowed[:half_rows, :half_rows],
        attn_part[:half_rows],
        log_part[:, :half_rows],
        grad_part[:half_rows],
        factor,
    )

    def later_block(bucket_id):
        first_key = bucket_id * key_step

        def run_block(operands):
            query_late, key_all, value_all, attn_late, log_late, grad_late = operands
            late_query, late_key, late_value = block_backward(
                query_late,
                key_all[first_key:],
                value_all[first_key:],
                allowed[half_rows:, first_key:],
                attn_late,
                log_late,
                grad_late,
                factor,
            )
            return (
                late_query,
                jnp.pad(late_key, ((first_key, 0), (0, 0))),
                jnp.pad(late_value, ((first_key, 0), (0, 0))),
            )

        return run_block

    late_query, late_key, late_value = lax.switch(
        bucket,
        [later_block(bucket_id) for bucket_id in range(5)],
        (
            query_part[half_rows:],
            key_part,
            value_part,
            attn_part[half_rows:],
            log_part[:, half_rows:],
            grad_part[half_rows:],
        ),
    )
    tail_rows = row_count - half_rows
    key_total = late_key + jnp.pad(early_key, ((0, tail_rows), (0, 0)))
    value_total = late_value + jnp.pad(early_value, ((0, tail_rows), (0, 0)))
    query_out = (
        jnp.concatenate([early_query, late_query], axis=0)
        .astype(jnp.bfloat16)
        .reshape(row_count, group_size * HEAD_SIZE)
    )
    return (query_out, key_total.astype(jnp.bfloat16), value_total.astype(jnp.bfloat16))


def pack_backward(query, keys, values, doc_ids, attn_rows, log_rows, grad_rows, factor):
    layout = pack_layout(doc_ids)
    parts = []
    for head_cluster in range(keys.shape[1] // HEAD_SIZE):
        parts.append(
            cluster_backward(
                head_cluster, query, keys, values, layout, attn_rows, log_rows, grad_rows, factor
            )
        )
    return tuple(jnp.concatenate([part[k] for part in parts], axis=1) for k in range(3))


def layer(query, keys, values, out_weight, loss_grad, lengths, languages, labels):
    factor = 1.0 / math.sqrt(HEAD_SIZE)
    row_count = query.shape[0]
    doc_ids = token_docs(lengths[0], row_count)
    attention_result, log_rows = pack_forward(query, keys, values, doc_ids, factor)
    token_lang = jnp.sum(
        jnp.where(
            doc_ids[:, None] == jnp.arange(DOCS, dtype=jnp.int32)[None, :], languages[0][None, :], 0
        ),
        axis=1,
    )
    counted = labels != -100
    lang_match = token_lang[:, None] == jnp.arange(LANGS, dtype=jnp.int32)[None, :]
    local_counts = jnp.sum((lang_match & counted[:, None]).astype(jnp.int32), axis=0)
    padded_counts = jnp.pad(local_counts, (0, 128 - LANGS))[None, :]
    counts = jnp.sum(lax.all_gather(padded_counts, "dp", axis=0, tiled=True), axis=0)[:LANGS].astype(
        jnp.float32
    )
    lang_weight = jnp.sqrt(jnp.sum(counts) / (LANGS * jnp.maximum(counts, 1.0)))
    token_weight = jnp.where(
        counted, jnp.sum(jnp.where(lang_match, lang_weight[None, :], 0.0), axis=1), 0.0
    )
    full_grad = lax.all_gather(loss_grad, "tensor", axis=1, tiled=True)
    weighted = (token_weight[:, None] * full_grad.astype(jnp.float32)).astype(jnp.bfloat16)
    out_grad = lax.dot_general(
        weighted,
        lax.all_gather(out_weight, "dp", axis=1, tiled=True),
        (((1,), (1,)), ((), ())),
        preferred_element_type=jnp.float32,
    ).astype(jnp.bfloat16)
    local_term = lax.dot_general(
        attention_result, weighted, (((0,), (0,)), ((), ())), preferred_element_type=jnp.float32
    )
    projection_part = lax.psum_scatter(
        local_term.astype(jnp.bfloat16), "dp", scatter_dimension=0, tiled=True
    )
    projection_gradient = lax.all_gather(projection_part, "dp", axis=0, tiled=True)
    query_gradient, key_gradient, value_gradient = pack_backward(
        query, keys, values, doc_ids, attention_result, log_rows, out_grad, factor
    )
    return (attention_result, query_gradient, key_gradient, value_gradient, projection_gradient)


def solution(mesh):
    in_specs = (
        P("dp", "tensor"),
        P("dp", "tensor"),
        P("dp", "tensor"),
        P("tensor", "dp"),
        P("dp", "tensor"),
        P("dp", None),
        P("dp", None),
        P("dp"),
    )
    out_specs = (
        P("dp", "tensor"),
        P("dp", "tensor"),
        P("dp", "tensor"),
        P("dp", "tensor"),
        P("tensor", None),
    )
    return jax.shard_map(layer, mesh=mesh, in_specs=in_specs, out_specs=out_specs, check_vma=False)
```

```python
import math

import jax
import jax.numpy as jnp
from jax import lax
from jax.sharding import PartitionSpec as P


QUERY_HEADS = 40
KEY_VALUE_HEADS = 8
HEAD_SIZE = 128
LANGS = 29
DOCS = 16


def token_docs(length_row, row_count):
    doc_ends = jnp.cumsum(length_row)
    places = jnp.arange(row_count, dtype=jnp.int32)
    return jnp.sum((places[:, None] >= doc_ends[None, :]).astype(jnp.int32), axis=1)


def masked_scores(query_rows, key_rows, allowed, factor):
    scores = (
        jnp.einsum("rgd,kd->grk", query_rows, key_rows, preferred_element_type=jnp.float32) * factor
    )
    return jnp.where(allowed[None], scores, -1e30)


def block_forward(query_rows, key_rows, value_rows, allowed, factor):
    scores = masked_scores(query_rows, key_rows, allowed, factor)
    row_top = jnp.max(scores, axis=2, keepdims=True)
    log_total = row_top + jnp.log(jnp.sum(jnp.exp(scores - row_top), axis=2, keepdims=True))
    weights = jnp.exp(scores - log_total).astype(jnp.bfloat16)
    result = jnp.einsum("grk,kd->rgd", weights, value_rows, preferred_element_type=jnp.float32)
    return (result.astype(jnp.bfloat16), log_total[:, :, 0])


def block_backward(
    query_rows, key_rows, value_rows, allowed, out_rows, log_rows, grad_rows, factor
):
    scores = masked_scores(query_rows, key_rows, allowed, factor)
    weights = jnp.exp(scores - log_rows[:, :, None])
    value_gradient = jnp.einsum(
        "grk,rgd->kd", weights.astype(jnp.bfloat16), grad_rows, preferred_element_type=jnp.float32
    )
    weight_grad = jnp.einsum(
        "rgd,kd->grk", grad_rows, value_rows, preferred_element_type=jnp.float32
    )
    diagonal_term = jnp.einsum(
        "rgd,rgd->gr", grad_rows, out_rows, preferred_element_type=jnp.float32
    )
    score_grad = (weights * (weight_grad - diagonal_term[:, :, None]) * factor).astype(jnp.bfloat16)
    query_gradient = jnp.einsum(
        "grk,kd->rgd", score_grad, key_rows, preferred_element_type=jnp.float32
    )
    key_gradient = jnp.einsum(
        "grk,rgd->kd", score_grad, query_rows, preferred_element_type=jnp.float32
    )
    return (query_gradient, key_gradient, value_gradient)


def pack_layout(doc_ids):
    row_count = doc_ids.shape[0]
    places = jnp.arange(row_count, dtype=jnp.int32)
    allowed = (doc_ids[:, None] == doc_ids[None, :]) & (places[:, None] >= places[None, :])
    half_rows = row_count // 2
    key_step = row_count // 8
    first_row = jnp.min(jnp.where(doc_ids == doc_ids[half_rows], places, row_count))
    return (allowed, half_rows, key_step, first_row // key_step)


def pack_forward(query, keys, values, doc_ids, factor):
    allowed, half_rows, key_step, bucket = pack_layout(doc_ids)
    row_count = doc_ids.shape[0]
    group_size = QUERY_HEADS // KEY_VALUE_HEADS
    outs = []
    logs = []
    for head_cluster in range(keys.shape[1] // HEAD_SIZE):
        query_part = query[
            :, head_cluster * group_size * HEAD_SIZE : (head_cluster + 1) * group_size * HEAD_SIZE
        ].reshape(row_count, group_size, HEAD_SIZE)
        key_part = keys[:, head_cluster * HEAD_SIZE : (head_cluster + 1) * HEAD_SIZE]
        value_part = values[:, head_cluster * HEAD_SIZE : (head_cluster + 1) * HEAD_SIZE]
        early_out, early_log = block_forward(
            query_part[:half_rows],
            key_part[:half_rows],
            value_part[:half_rows],
            allowed[:half_rows, :half_rows],
            factor,
        )

        def later_block(bucket_id):
            first_key = bucket_id * key_step

            def run_block(operands):
                query_late, key_all, value_all = operands
                return block_forward(
                    query_late,
                    key_all[first_key:],
                    value_all[first_key:],
                    allowed[half_rows:, first_key:],
                    factor,
                )

            return run_block

        late_out, late_log = lax.switch(
            bucket,
            [later_block(bucket_id) for bucket_id in range(5)],
            (query_part[half_rows:], key_part, value_part),
        )
        outs.append(
            jnp.concatenate([early_out, late_out], axis=0).reshape(
                row_count, group_size * HEAD_SIZE
            )
        )
        logs.append(jnp.concatenate([early_log, late_log], axis=1))
    return (jnp.concatenate(outs, axis=1), jnp.stack(logs, axis=0))


def cluster_backward(
    head_cluster, query, keys, values, layout, attn_rows, log_rows, grad_rows, factor
):
    allowed, half_rows, key_step, bucket = layout
    row_count = query.shape[0]
    group_size = QUERY_HEADS // KEY_VALUE_HEADS
    span = slice(
        head_cluster * group_size * HEAD_SIZE, (head_cluster + 1) * group_size * HEAD_SIZE
    )
    query_part = query[:, span].reshape(row_count, group_size, HEAD_SIZE)
    attn_part = attn_rows[:, span].reshape(row_count, group_size, HEAD_SIZE)
    grad_part = grad_rows[:, span].reshape(row_count, group_size, HEAD_SIZE)
    key_part = keys[:, head_cluster * HEAD_SIZE : (head_cluster + 1) * HEAD_SIZE]
    value_part = values[:, head_cluster * HEAD_SIZE : (head_cluster + 1) * HEAD_SIZE]
    log_part = log_rows[head_cluster]
    early_query, early_key, early_value = block_backward(
        query_part[:half_rows],
        key_part[:half_rows],
        value_part[:half_rows],
        allowed[:half_rows, :half_rows],
        attn_part[:half_rows],
        log_part[:, :half_rows],
        grad_part[:half_rows],
        factor,
    )

    def later_block(bucket_id):
        first_key = bucket_id * key_step

        def run_block(operands):
            query_late, key_all, value_all, attn_late, log_late, grad_late = operands
            late_query, late_key, late_value = block_backward(
                query_late,
                key_all[first_key:],
                value_all[first_key:],
                allowed[half_rows:, first_key:],
                attn_late,
                log_late,
                grad_late,
                factor,
            )
            return (
                late_query,
                jnp.pad(late_key, ((first_key, 0), (0, 0))),
                jnp.pad(late_value, ((first_key, 0), (0, 0))),
            )

        return run_block

    late_query, late_key, late_value = lax.switch(
        bucket,
        [later_block(bucket_id) for bucket_id in range(5)],
        (
            query_part[half_rows:],
            key_part,
            value_part,
            attn_part[half_rows:],
            log_part[:, half_rows:],
            grad_part[half_rows:],
        ),
    )
    tail_rows = row_count - half_rows
    key_total = late_key + jnp.pad(early_key, ((0, tail_rows), (0, 0)))
    value_total = late_value + jnp.pad(early_value, ((0, tail_rows), (0, 0)))
    query_out = (
        jnp.concatenate([early_query, late_query], axis=0)
        .astype(jnp.bfloat16)
        .reshape(row_count, group_size * HEAD_SIZE)
    )
    return (query_out, key_total.astype(jnp.bfloat16), value_total.astype(jnp.bfloat16))


def pack_backward(query, keys, values, doc_ids, attn_rows, log_rows, grad_rows, factor):
    layout = pack_layout(doc_ids)
    parts = []
    for head_cluster in range(keys.shape[1] // HEAD_SIZE):
        parts.append(
            cluster_backward(
                head_cluster, query, keys, values, layout, attn_rows, log_rows, grad_rows, factor
            )
        )
    return tuple(jnp.concatenate([part[k] for part in parts], axis=1) for k in range(3))


def gather_features(block):
    tensor_size = lax.axis_size("tensor")
    me = lax.axis_index("tensor")
    arrived = [block]
    for shift in range(1, tensor_size):
        pairs = [(index, (index + shift) % tensor_size) for index in range(tensor_size)]
        arrived.append(lax.ppermute(block, "tensor", pairs))
    stacked = jnp.stack(arrived)
    order = (me - jnp.arange(tensor_size, dtype=jnp.int32)) % tensor_size
    ordered = jnp.take(stacked, order, axis=0)
    return ordered.transpose(1, 0, 2).reshape(block.shape[0], tensor_size * block.shape[1])


def layer(query, keys, values, out_weight, loss_grad, lengths, languages, labels):
    factor = 1.0 / math.sqrt(HEAD_SIZE)
    row_count = query.shape[0]
    doc_ids = token_docs(lengths[0], row_count)
    attention_result, log_rows = pack_forward(query, keys, values, doc_ids, factor)
    token_lang = jnp.sum(
        jnp.where(
            doc_ids[:, None] == jnp.arange(DOCS, dtype=jnp.int32)[None, :], languages[0][None, :], 0
        ),
        axis=1,
    )
    counted = labels != -100
    lang_match = token_lang[:, None] == jnp.arange(LANGS, dtype=jnp.int32)[None, :]
    local_counts = jnp.sum((lang_match & counted[:, None]).astype(jnp.int32), axis=0)
    dp_size = lax.axis_size("dp")
    total_counts = local_counts
    step = 1
    while step < dp_size:
        pairs = [(index, index ^ step) for index in range(dp_size)]
        total_counts = total_counts + lax.ppermute(total_counts, "dp", pairs)
        step *= 2
    counts = total_counts.astype(jnp.float32)
    lang_weight = jnp.sqrt(jnp.sum(counts) / (LANGS * jnp.maximum(counts, 1.0)))
    token_weight = jnp.where(
        counted, jnp.sum(jnp.where(lang_match, lang_weight[None, :], 0.0), axis=1), 0.0
    )
    full_grad = gather_features(loss_grad)
    weighted = (token_weight[:, None] * full_grad.astype(jnp.float32)).astype(jnp.bfloat16)
    out_grad = lax.dot_general(
        weighted,
        lax.all_gather(out_weight, "dp", axis=1, tiled=True),
        (((1,), (1,)), ((), ())),
        preferred_element_type=jnp.float32,
    ).astype(jnp.bfloat16)
    local_term = lax.dot_general(
        attention_result, weighted, (((0,), (0,)), ((), ())), preferred_element_type=jnp.float32
    )
    projection_part = lax.psum_scatter(
        local_term.astype(jnp.bfloat16), "dp", scatter_dimension=0, tiled=True
    )
    projection_gradient = lax.all_gather(projection_part, "dp", axis=0, tiled=True)
    query_gradient, key_gradient, value_gradient = pack_backward(
        query, keys, values, doc_ids, attention_result, log_rows, out_grad, factor
    )
    return (attention_result, query_gradient, key_gradient, value_gradient, projection_gradient)


def solution(mesh):
    in_specs = (
        P("dp", "tensor"),
        P("dp", "tensor"),
        P("dp", "tensor"),
        P("tensor", "dp"),
        P("dp", "tensor"),
        P("dp", None),
        P("dp", None),
        P("dp"),
    )
    out_specs = (
        P("dp", "tensor"),
        P("dp", "tensor"),
        P("dp", "tensor"),
        P("dp", "tensor"),
        P("tensor", None),
    )
    return jax.shard_map(layer, mesh=mesh, in_specs=in_specs, out_specs=out_specs, check_vma=False)
```

```python
import math

import jax
import jax.numpy as jnp
from jax import lax
from jax.sharding import PartitionSpec as P


QUERY_HEADS = 40
KEY_VALUE_HEADS = 8
HEAD_SIZE = 128
LANGS = 29
DOCS = 16


def token_docs(length_row, row_count):
    doc_ends = jnp.cumsum(length_row)
    places = jnp.arange(row_count, dtype=jnp.int32)
    return jnp.sum((places[:, None] >= doc_ends[None, :]).astype(jnp.int32), axis=1)


def masked_scores(query_rows, key_rows, allowed, factor):
    scores = (
        jnp.einsum("rgd,kd->grk", query_rows, key_rows, preferred_element_type=jnp.float32) * factor
    )
    return jnp.where(allowed[None], scores, -1e30)


def block_forward(query_rows, key_rows, value_rows, allowed, factor):
    scores = masked_scores(query_rows, key_rows, allowed, factor)
    row_top = jnp.max(scores, axis=2, keepdims=True)
    log_total = row_top + jnp.log(jnp.sum(jnp.exp(scores - row_top), axis=2, keepdims=True))
    weights = jnp.exp(scores - log_total).astype(jnp.bfloat16)
    result = jnp.einsum("grk,kd->rgd", weights, value_rows, preferred_element_type=jnp.float32)
    return (result.astype(jnp.bfloat16), log_total[:, :, 0])


def block_backward(
    query_rows, key_rows, value_rows, allowed, out_rows, log_rows, grad_rows, factor
):
    scores = masked_scores(query_rows, key_rows, allowed, factor)
    weights = jnp.exp(scores - log_rows[:, :, None])
    value_gradient = jnp.einsum(
        "grk,rgd->kd", weights.astype(jnp.bfloat16), grad_rows, preferred_element_type=jnp.float32
    )
    weight_grad = jnp.einsum(
        "rgd,kd->grk", grad_rows, value_rows, preferred_element_type=jnp.float32
    )
    diagonal_term = jnp.einsum(
        "rgd,rgd->gr", grad_rows, out_rows, preferred_element_type=jnp.float32
    )
    score_grad = (weights * (weight_grad - diagonal_term[:, :, None]) * factor).astype(jnp.bfloat16)
    query_gradient = jnp.einsum(
        "grk,kd->rgd", score_grad, key_rows, preferred_element_type=jnp.float32
    )
    key_gradient = jnp.einsum(
        "grk,rgd->kd", score_grad, query_rows, preferred_element_type=jnp.float32
    )
    return (query_gradient, key_gradient, value_gradient)


def pack_layout(doc_ids):
    row_count = doc_ids.shape[0]
    places = jnp.arange(row_count, dtype=jnp.int32)
    allowed = (doc_ids[:, None] == doc_ids[None, :]) & (places[:, None] >= places[None, :])
    half_rows = row_count // 2
    key_step = row_count // 8
    first_row = jnp.min(jnp.where(doc_ids == doc_ids[half_rows], places, row_count))
    return (allowed, half_rows, key_step, first_row // key_step)


def pack_forward(query, keys, values, doc_ids, factor):
    allowed, half_rows, key_step, bucket = pack_layout(doc_ids)
    row_count = doc_ids.shape[0]
    group_size = QUERY_HEADS // KEY_VALUE_HEADS
    outs = []
    logs = []
    for head_cluster in range(keys.shape[1] // HEAD_SIZE):
        query_part = query[
            :, head_cluster * group_size * HEAD_SIZE : (head_cluster + 1) * group_size * HEAD_SIZE
        ].reshape(row_count, group_size, HEAD_SIZE)
        key_part = keys[:, head_cluster * HEAD_SIZE : (head_cluster + 1) * HEAD_SIZE]
        value_part = values[:, head_cluster * HEAD_SIZE : (head_cluster + 1) * HEAD_SIZE]
        early_out, early_log = block_forward(
            query_part[:half_rows],
            key_part[:half_rows],
            value_part[:half_rows],
            allowed[:half_rows, :half_rows],
            factor,
        )

        def later_block(bucket_id):
            first_key = bucket_id * key_step

            def run_block(operands):
                query_late, key_all, value_all = operands
                return block_forward(
                    query_late,
                    key_all[first_key:],
                    value_all[first_key:],
                    allowed[half_rows:, first_key:],
                    factor,
                )

            return run_block

        late_out, late_log = lax.switch(
            bucket,
            [later_block(bucket_id) for bucket_id in range(5)],
            (query_part[half_rows:], key_part, value_part),
        )
        outs.append(
            jnp.concatenate([early_out, late_out], axis=0).reshape(
                row_count, group_size * HEAD_SIZE
            )
        )
        logs.append(jnp.concatenate([early_log, late_log], axis=1))
    return (jnp.concatenate(outs, axis=1), jnp.stack(logs, axis=0))


def cluster_backward(
    head_cluster, query, keys, values, layout, attn_rows, log_rows, grad_rows, factor
):
    allowed, half_rows, key_step, bucket = layout
    row_count = query.shape[0]
    group_size = QUERY_HEADS // KEY_VALUE_HEADS
    span = slice(
        head_cluster * group_size * HEAD_SIZE, (head_cluster + 1) * group_size * HEAD_SIZE
    )
    query_part = query[:, span].reshape(row_count, group_size, HEAD_SIZE)
    attn_part = attn_rows[:, span].reshape(row_count, group_size, HEAD_SIZE)
    grad_part = grad_rows[:, span].reshape(row_count, group_size, HEAD_SIZE)
    key_part = keys[:, head_cluster * HEAD_SIZE : (head_cluster + 1) * HEAD_SIZE]
    value_part = values[:, head_cluster * HEAD_SIZE : (head_cluster + 1) * HEAD_SIZE]
    log_part = log_rows[head_cluster]
    early_query, early_key, early_value = block_backward(
        query_part[:half_rows],
        key_part[:half_rows],
        value_part[:half_rows],
        allowed[:half_rows, :half_rows],
        attn_part[:half_rows],
        log_part[:, :half_rows],
        grad_part[:half_rows],
        factor,
    )

    def later_block(bucket_id):
        first_key = bucket_id * key_step

        def run_block(operands):
            query_late, key_all, value_all, attn_late, log_late, grad_late = operands
            late_query, late_key, late_value = block_backward(
                query_late,
                key_all[first_key:],
                value_all[first_key:],
                allowed[half_rows:, first_key:],
                attn_late,
                log_late,
                grad_late,
                factor,
            )
            return (
                late_query,
                jnp.pad(late_key, ((first_key, 0), (0, 0))),
                jnp.pad(late_value, ((first_key, 0), (0, 0))),
            )

        return run_block

    late_query, late_key, late_value = lax.switch(
        bucket,
        [later_block(bucket_id) for bucket_id in range(5)],
        (
            query_part[half_rows:],
            key_part,
            value_part,
            attn_part[half_rows:],
            log_part[:, half_rows:],
            grad_part[half_rows:],
        ),
    )
    tail_rows = row_count - half_rows
    key_total = late_key + jnp.pad(early_key, ((0, tail_rows), (0, 0)))
    value_total = late_value + jnp.pad(early_value, ((0, tail_rows), (0, 0)))
    query_out = (
        jnp.concatenate([early_query, late_query], axis=0)
        .astype(jnp.bfloat16)
        .reshape(row_count, group_size * HEAD_SIZE)
    )
    return (query_out, key_total.astype(jnp.bfloat16), value_total.astype(jnp.bfloat16))


def pack_backward(query, keys, values, doc_ids, attn_rows, log_rows, grad_rows, factor):
    layout = pack_layout(doc_ids)
    parts = []
    for head_cluster in range(keys.shape[1] // HEAD_SIZE):
        parts.append(
            cluster_backward(
                head_cluster, query, keys, values, layout, attn_rows, log_rows, grad_rows, factor
            )
        )
    return tuple(jnp.concatenate([part[k] for part in parts], axis=1) for k in range(3))


def gather_features(block):
    tensor_size = lax.axis_size("tensor")
    me = lax.axis_index("tensor")
    arrived = [block]
    for shift in range(1, tensor_size):
        pairs = [(index, (index + shift) % tensor_size) for index in range(tensor_size)]
        arrived.append(lax.ppermute(block, "tensor", pairs))
    width = block.shape[1]
    full = jnp.zeros((block.shape[0], tensor_size * width), block.dtype)
    for shift, part in enumerate(arrived):
        source = (me - shift) % tensor_size
        full = lax.dynamic_update_slice(full, part, (0, source * width))
    return full


def layer(query, keys, values, out_weight, loss_grad, lengths, languages, labels):
    factor = 1.0 / math.sqrt(HEAD_SIZE)
    row_count = query.shape[0]
    doc_ids = token_docs(lengths[0], row_count)
    attention_result, log_rows = pack_forward(query, keys, values, doc_ids, factor)
    token_lang = jnp.sum(
        jnp.where(
            doc_ids[:, None] == jnp.arange(DOCS, dtype=jnp.int32)[None, :], languages[0][None, :], 0
        ),
        axis=1,
    )
    counted = labels != -100
    lang_match = token_lang[:, None] == jnp.arange(LANGS, dtype=jnp.int32)[None, :]
    local_counts = jnp.sum((lang_match & counted[:, None]).astype(jnp.int32), axis=0)
    dp_size = lax.axis_size("dp")
    total_counts = local_counts
    step = 1
    while step < dp_size:
        pairs = [(index, index ^ step) for index in range(dp_size)]
        total_counts = total_counts + lax.ppermute(total_counts, "dp", pairs)
        step *= 2
    counts = total_counts.astype(jnp.float32)
    lang_weight = jnp.sqrt(jnp.sum(counts) / (LANGS * jnp.maximum(counts, 1.0)))
    token_weight = jnp.where(
        counted, jnp.sum(jnp.where(lang_match, lang_weight[None, :], 0.0), axis=1), 0.0
    )
    full_grad = gather_features(loss_grad)
    weighted = (token_weight[:, None] * full_grad.astype(jnp.float32)).astype(jnp.bfloat16)
    local_term = lax.dot_general(
        attention_result, weighted, (((0,), (0,)), ((), ())), preferred_element_type=jnp.float32
    )
    projection_part = lax.psum_scatter(
        local_term.astype(jnp.bfloat16), "dp", scatter_dimension=0, tiled=True
    )
    projection_gradient = lax.all_gather(projection_part, "dp", axis=0, tiled=True)
    local_term, weighted = lax.optimization_barrier((local_term, weighted))
    out_grad = lax.dot_general(
        weighted,
        lax.all_gather(out_weight, "dp", axis=1, tiled=True),
        (((1,), (1,)), ((), ())),
        preferred_element_type=jnp.float32,
    ).astype(jnp.bfloat16)

    query_gradient, key_gradient, value_gradient = pack_backward(
        query, keys, values, doc_ids, attention_result, log_rows, out_grad, factor
    )
    return (attention_result, query_gradient, key_gradient, value_gradient, projection_gradient)


def solution(mesh):
    in_specs = (
        P("dp", "tensor"),
        P("dp", "tensor"),
        P("dp", "tensor"),
        P("tensor", "dp"),
        P("dp", "tensor"),
        P("dp", None),
        P("dp", None),
        P("dp"),
    )
    out_specs = (
        P("dp", "tensor"),
        P("dp", "tensor"),
        P("dp", "tensor"),
        P("dp", "tensor"),
        P("tensor", None),
    )
    return jax.shard_map(layer, mesh=mesh, in_specs=in_specs, out_specs=out_specs, check_vma=False)
```

```python
import math

import jax
import jax.numpy as jnp
from jax import lax
from jax.sharding import PartitionSpec as P


QUERY_HEADS = 40
KEY_VALUE_HEADS = 8
HEAD_SIZE = 128
LANGS = 29
DOCS = 16
COUNT_BASE = 32


def token_docs(length_row, row_count):
    doc_ends = jnp.cumsum(length_row)
    places = jnp.arange(row_count, dtype=jnp.int32)
    return jnp.sum((places[:, None] >= doc_ends[None, :]).astype(jnp.int32), axis=1)


def masked_scores(query_rows, key_rows, allowed, factor):
    scores = (
        jnp.einsum("rgd,kd->grk", query_rows, key_rows, preferred_element_type=jnp.float32) * factor
    )
    return jnp.where(allowed[None], scores, -1e30)


def block_forward(query_rows, key_rows, value_rows, allowed, factor):
    scores = masked_scores(query_rows, key_rows, allowed, factor)
    row_top = jnp.max(scores, axis=2, keepdims=True)
    log_total = row_top + jnp.log(jnp.sum(jnp.exp(scores - row_top), axis=2, keepdims=True))
    weights = jnp.exp(scores - log_total).astype(jnp.bfloat16)
    result = jnp.einsum("grk,kd->rgd", weights, value_rows, preferred_element_type=jnp.float32)
    return (result.astype(jnp.bfloat16), log_total[:, :, 0])


def block_backward(
    query_rows, key_rows, value_rows, allowed, out_rows, log_rows, grad_rows, factor
):
    scores = masked_scores(query_rows, key_rows, allowed, factor)
    weights = jnp.exp(scores - log_rows[:, :, None])
    value_gradient = jnp.einsum(
        "grk,rgd->kd", weights.astype(jnp.bfloat16), grad_rows, preferred_element_type=jnp.float32
    )
    weight_grad = jnp.einsum(
        "rgd,kd->grk", grad_rows, value_rows, preferred_element_type=jnp.float32
    )
    diagonal_term = jnp.einsum(
        "rgd,rgd->gr", grad_rows, out_rows, preferred_element_type=jnp.float32
    )
    score_grad = (weights * (weight_grad - diagonal_term[:, :, None]) * factor).astype(jnp.bfloat16)
    query_gradient = jnp.einsum(
        "grk,kd->rgd", score_grad, key_rows, preferred_element_type=jnp.float32
    )
    key_gradient = jnp.einsum(
        "grk,rgd->kd", score_grad, query_rows, preferred_element_type=jnp.float32
    )
    return (query_gradient, key_gradient, value_gradient)


def pack_layout(doc_ids):
    row_count = doc_ids.shape[0]
    places = jnp.arange(row_count, dtype=jnp.int32)
    allowed = (doc_ids[:, None] == doc_ids[None, :]) & (places[:, None] >= places[None, :])
    half_rows = row_count // 2
    key_step = row_count // 8
    first_row = jnp.min(jnp.where(doc_ids == doc_ids[half_rows], places, row_count))
    return (allowed, half_rows, key_step, first_row // key_step)


def pack_forward(query, keys, values, doc_ids, factor):
    allowed, half_rows, key_step, bucket = pack_layout(doc_ids)
    row_count = doc_ids.shape[0]
    group_size = QUERY_HEADS // KEY_VALUE_HEADS
    outs = []
    logs = []
    for head_cluster in range(keys.shape[1] // HEAD_SIZE):
        query_part = query[
            :, head_cluster * group_size * HEAD_SIZE : (head_cluster + 1) * group_size * HEAD_SIZE
        ].reshape(row_count, group_size, HEAD_SIZE)
        key_part = keys[:, head_cluster * HEAD_SIZE : (head_cluster + 1) * HEAD_SIZE]
        value_part = values[:, head_cluster * HEAD_SIZE : (head_cluster + 1) * HEAD_SIZE]
        early_out, early_log = block_forward(
            query_part[:half_rows],
            key_part[:half_rows],
            value_part[:half_rows],
            allowed[:half_rows, :half_rows],
            factor,
        )

        def later_block(bucket_id):
            first_key = bucket_id * key_step

            def run_block(operands):
                query_late, key_all, value_all = operands
                return block_forward(
                    query_late,
                    key_all[first_key:],
                    value_all[first_key:],
                    allowed[half_rows:, first_key:],
                    factor,
                )

            return run_block

        late_out, late_log = lax.switch(
            bucket,
            [later_block(bucket_id) for bucket_id in range(5)],
            (query_part[half_rows:], key_part, value_part),
        )
        outs.append(
            jnp.concatenate([early_out, late_out], axis=0).reshape(
                row_count, group_size * HEAD_SIZE
            )
        )
        logs.append(jnp.concatenate([early_log, late_log], axis=1))
    return (jnp.concatenate(outs, axis=1), jnp.stack(logs, axis=0))


def cluster_backward(
    head_cluster, query, keys, values, layout, attn_rows, log_rows, grad_rows, factor
):
    allowed, half_rows, key_step, bucket = layout
    row_count = query.shape[0]
    group_size = QUERY_HEADS // KEY_VALUE_HEADS
    span = slice(
        head_cluster * group_size * HEAD_SIZE, (head_cluster + 1) * group_size * HEAD_SIZE
    )
    query_part = query[:, span].reshape(row_count, group_size, HEAD_SIZE)
    attn_part = attn_rows[:, span].reshape(row_count, group_size, HEAD_SIZE)
    grad_part = grad_rows[:, span].reshape(row_count, group_size, HEAD_SIZE)
    key_part = keys[:, head_cluster * HEAD_SIZE : (head_cluster + 1) * HEAD_SIZE]
    value_part = values[:, head_cluster * HEAD_SIZE : (head_cluster + 1) * HEAD_SIZE]
    log_part = log_rows[head_cluster]
    early_query, early_key, early_value = block_backward(
        query_part[:half_rows],
        key_part[:half_rows],
        value_part[:half_rows],
        allowed[:half_rows, :half_rows],
        attn_part[:half_rows],
        log_part[:, :half_rows],
        grad_part[:half_rows],
        factor,
    )

    def later_block(bucket_id):
        first_key = bucket_id * key_step

        def run_block(operands):
            query_late, key_all, value_all, attn_late, log_late, grad_late = operands
            late_query, late_key, late_value = block_backward(
                query_late,
                key_all[first_key:],
                value_all[first_key:],
                allowed[half_rows:, first_key:],
                attn_late,
                log_late,
                grad_late,
                factor,
            )
            return (
                late_query,
                jnp.pad(late_key, ((first_key, 0), (0, 0))),
                jnp.pad(late_value, ((first_key, 0), (0, 0))),
            )

        return run_block

    late_query, late_key, late_value = lax.switch(
        bucket,
        [later_block(bucket_id) for bucket_id in range(5)],
        (
            query_part[half_rows:],
            key_part,
            value_part,
            attn_part[half_rows:],
            log_part[:, half_rows:],
            grad_part[half_rows:],
        ),
    )
    tail_rows = row_count - half_rows
    key_total = late_key + jnp.pad(early_key, ((0, tail_rows), (0, 0)))
    value_total = late_value + jnp.pad(early_value, ((0, tail_rows), (0, 0)))
    query_out = (
        jnp.concatenate([early_query, late_query], axis=0)
        .astype(jnp.bfloat16)
        .reshape(row_count, group_size * HEAD_SIZE)
    )
    return (query_out, key_total.astype(jnp.bfloat16), value_total.astype(jnp.bfloat16))


def pack_backward(query, keys, values, doc_ids, attn_rows, log_rows, grad_rows, factor):
    layout = pack_layout(doc_ids)
    parts = []
    for head_cluster in range(keys.shape[1] // HEAD_SIZE):
        parts.append(
            cluster_backward(
                head_cluster, query, keys, values, layout, attn_rows, log_rows, grad_rows, factor
            )
        )
    return tuple(jnp.concatenate([part[k] for part in parts], axis=1) for k in range(3))


def attach_counts(out_weight, local_counts):
    high = (local_counts // COUNT_BASE).astype(out_weight.dtype)
    low = (local_counts % COUNT_BASE).astype(out_weight.dtype)
    rows = jnp.zeros((16, out_weight.shape[1]), out_weight.dtype)
    rows = rows.at[0, :LANGS].set(high).at[1, :LANGS].set(low)
    return jnp.concatenate([out_weight, rows], axis=0)


def gather_features(block):
    tensor_size = lax.axis_size("tensor")
    me = lax.axis_index("tensor")
    arrived = [block]
    for shift in range(1, tensor_size):
        pairs = [(index, (index + shift) % tensor_size) for index in range(tensor_size)]
        arrived.append(lax.ppermute(block, "tensor", pairs))
    width = block.shape[1]
    full = jnp.zeros((block.shape[0], tensor_size * width), block.dtype)
    for shift, part in enumerate(arrived):
        source = (me - shift) % tensor_size
        full = lax.dynamic_update_slice(full, part, (0, source * width))
    return full


def layer(query, keys, values, out_weight, loss_grad, lengths, languages, labels):
    factor = 1.0 / math.sqrt(HEAD_SIZE)
    row_count = query.shape[0]
    doc_ids = token_docs(lengths[0], row_count)
    attention_result, log_rows = pack_forward(query, keys, values, doc_ids, factor)
    token_lang = jnp.sum(
        jnp.where(
            doc_ids[:, None] == jnp.arange(DOCS, dtype=jnp.int32)[None, :], languages[0][None, :], 0
        ),
        axis=1,
    )
    counted = labels != -100
    lang_match = token_lang[:, None] == jnp.arange(LANGS, dtype=jnp.int32)[None, :]
    local_counts = jnp.sum((lang_match & counted[:, None]).astype(jnp.int32), axis=0)
    weight_rows = out_weight.shape[0]
    gathered = lax.all_gather(attach_counts(out_weight, local_counts), "dp", axis=1, tiled=True)
    full_weight = gathered[:weight_rows]
    code = gathered[weight_rows : weight_rows + 2].astype(jnp.float32)
    code = code.reshape(2, lax.axis_size("dp"), out_weight.shape[1])[:, :, :LANGS]
    counts = jnp.sum(code[0] * COUNT_BASE + code[1], axis=0)
    lang_weight = jnp.sqrt(jnp.sum(counts) / (LANGS * jnp.maximum(counts, 1.0)))
    token_weight = jnp.where(
        counted, jnp.sum(jnp.where(lang_match, lang_weight[None, :], 0.0), axis=1), 0.0
    )
    full_grad = gather_features(loss_grad)
    weighted = (token_weight[:, None] * full_grad.astype(jnp.float32)).astype(jnp.bfloat16)
    local_term = lax.dot_general(
        attention_result, weighted, (((0,), (0,)), ((), ())), preferred_element_type=jnp.float32
    )
    projection_part = lax.psum_scatter(
        local_term.astype(jnp.bfloat16), "dp", scatter_dimension=0, tiled=True
    )
    projection_gradient = lax.all_gather(projection_part, "dp", axis=0, tiled=True)
    local_term, weighted = lax.optimization_barrier((local_term, weighted))
    out_grad = lax.dot_general(
        weighted,
        full_weight,
        (((1,), (1,)), ((), ())),
        preferred_element_type=jnp.float32,
    ).astype(jnp.bfloat16)

    query_gradient, key_gradient, value_gradient = pack_backward(
        query, keys, values, doc_ids, attention_result, log_rows, out_grad, factor
    )
    return (attention_result, query_gradient, key_gradient, value_gradient, projection_gradient)


def solution(mesh):
    in_specs = (
        P("dp", "tensor"),
        P("dp", "tensor"),
        P("dp", "tensor"),
        P("tensor", "dp"),
        P("dp", "tensor"),
        P("dp", None),
        P("dp", None),
        P("dp"),
    )
    out_specs = (
        P("dp", "tensor"),
        P("dp", "tensor"),
        P("dp", "tensor"),
        P("dp", "tensor"),
        P("tensor", None),
    )
    return jax.shard_map(layer, mesh=mesh, in_specs=in_specs, out_specs=out_specs, check_vma=False)
```

```python
import functools
import math

import jax
import jax.numpy as jnp
from jax import lax
from jax.experimental import pallas as pl
from jax.experimental.pallas import tpu as pltpu
from jax.sharding import PartitionSpec as P


QUERY_HEADS = 40
KEY_VALUE_HEADS = 8
HEAD_SIZE = 128
LANGS = 29
DOCS = 16
COUNT_BASE = 32


def token_docs(length_row, row_count):
    doc_ends = jnp.cumsum(length_row)
    places = jnp.arange(row_count, dtype=jnp.int32)
    return jnp.sum((places[:, None] >= doc_ends[None, :]).astype(jnp.int32), axis=1)


GROUP = QUERY_HEADS // KEY_VALUE_HEADS
ROW_BLOCK = 256
MASKED = -1e30
NT_DIMS = (((1,), (1,)), ((), ()))


def block_mask(row_doc_ref, col_doc_ref, first_row, key_end):
    row_doc = row_doc_ref[first_row : first_row + ROW_BLOCK, :]
    col_doc = col_doc_ref[:, :key_end]
    shape = (ROW_BLOCK, key_end)
    rows = lax.broadcasted_iota(jnp.int32, shape, 0) + first_row
    cols = lax.broadcasted_iota(jnp.int32, shape, 1)
    return (row_doc == col_doc) & (cols <= rows)


def forward_kernel(factor, q_ref, k_ref, v_ref, row_doc_ref, col_doc_ref, o_ref, lse_ref):
    row_count = q_ref.shape[0]
    for block in range(row_count // ROW_BLOCK):
        first_row = block * ROW_BLOCK
        key_end = first_row + ROW_BLOCK
        allowed = block_mask(row_doc_ref, col_doc_ref, first_row, key_end)
        rows = pl.ds(first_row, ROW_BLOCK)

        def head_body(head, carry):
            cols = pl.ds(pl.multiple_of(head * HEAD_SIZE, HEAD_SIZE), HEAD_SIZE)
            query = q_ref[rows, cols]
            scores = lax.dot_general(
                query, k_ref[:key_end, :], NT_DIMS, preferred_element_type=jnp.float32
            ) * factor
            scores = jnp.where(allowed, scores, MASKED)
            top = jnp.max(scores, axis=1, keepdims=True)
            log_total = top + jnp.log(jnp.sum(jnp.exp(scores - top), axis=1, keepdims=True))
            weights = jnp.exp(scores - log_total).astype(jnp.bfloat16)
            result = jnp.dot(weights, v_ref[:key_end, :], preferred_element_type=jnp.float32)
            o_ref[rows, cols] = result.astype(o_ref.dtype)
            lse_ref[0, head, rows, :] = jnp.broadcast_to(log_total, (ROW_BLOCK, HEAD_SIZE))
            return carry

        lax.fori_loop(0, GROUP, head_body, 0)


def backward_kernel(
    factor, q_ref, k_ref, v_ref, row_doc_ref, col_doc_ref, o_ref, do_ref, lse_ref,
    dq_ref, dk_ref, dv_ref, dk_acc, dv_acc,
):
    row_count = q_ref.shape[0]
    dk_acc[...] = jnp.zeros_like(dk_acc)
    dv_acc[...] = jnp.zeros_like(dv_acc)
    for block in range(row_count // ROW_BLOCK):
        first_row = block * ROW_BLOCK
        key_end = first_row + ROW_BLOCK
        allowed = block_mask(row_doc_ref, col_doc_ref, first_row, key_end)
        rows = pl.ds(first_row, ROW_BLOCK)

        def head_body(head, carry):
            cols = pl.ds(pl.multiple_of(head * HEAD_SIZE, HEAD_SIZE), HEAD_SIZE)
            query = q_ref[rows, cols]
            grad = do_ref[rows, cols]
            keys = k_ref[:key_end, :]
            values = v_ref[:key_end, :]
            log_total = lse_ref[0, head, rows, :][:, :1]
            scores = lax.dot_general(query, keys, NT_DIMS, preferred_element_type=jnp.float32) * factor
            scores = jnp.where(allowed, scores, MASKED)
            weights = jnp.exp(scores - log_total)
            dv_acc[:key_end, :] += jnp.dot(
                weights.astype(jnp.bfloat16).T, grad, preferred_element_type=jnp.float32
            )
            weight_grad = lax.dot_general(grad, values, NT_DIMS, preferred_element_type=jnp.float32)
            diagonal = jnp.sum(
                grad.astype(jnp.float32) * o_ref[rows, cols].astype(jnp.float32), axis=1, keepdims=True
            )
            score_grad = (weights * (weight_grad - diagonal) * factor).astype(jnp.bfloat16)
            dq_ref[rows, cols] = jnp.dot(score_grad, keys, preferred_element_type=jnp.float32).astype(
                dq_ref.dtype
            )
            dk_acc[:key_end, :] += jnp.dot(score_grad.T, query, preferred_element_type=jnp.float32)
            return carry

        lax.fori_loop(0, GROUP, head_body, 0)
    dk_ref[...] = dk_acc[...].astype(dk_ref.dtype)
    dv_ref[...] = dv_acc[...].astype(dv_ref.dtype)


def doc_views(doc_ids):
    return doc_ids[:, None], doc_ids[None, :]


def attention_forward(query, keys, values, doc_ids, factor):
    row_count = query.shape[0]
    groups = keys.shape[1] // HEAD_SIZE
    width = GROUP * HEAD_SIZE
    row_doc, col_doc = doc_views(doc_ids)
    flops = 4 * groups * GROUP * row_count * row_count * HEAD_SIZE
    return pl.pallas_call(
        functools.partial(forward_kernel, factor),
        grid=(groups,),
        in_specs=[
            pl.BlockSpec((row_count, width), lambda g: (0, g)),
            pl.BlockSpec((row_count, HEAD_SIZE), lambda g: (0, g)),
            pl.BlockSpec((row_count, HEAD_SIZE), lambda g: (0, g)),
            pl.BlockSpec((row_count, 1), lambda g: (0, 0)),
            pl.BlockSpec((1, row_count), lambda g: (0, 0)),
        ],
        out_specs=[
            pl.BlockSpec((row_count, width), lambda g: (0, g)),
            pl.BlockSpec((1, GROUP, row_count, HEAD_SIZE), lambda g: (g, 0, 0, 0)),
        ],
        out_shape=[
            jax.ShapeDtypeStruct(query.shape, query.dtype),
            jax.ShapeDtypeStruct((groups, GROUP, row_count, HEAD_SIZE), jnp.float32),
        ],
        compiler_params=pltpu.CompilerParams(vmem_limit_bytes=48 * 1024 * 1024),
        cost_estimate=pl.CostEstimate(
            flops=flops // 2, transcendentals=groups * GROUP * row_count * row_count // 2,
            bytes_accessed=4 * query.size + 8 * keys.size + 8 * groups * GROUP * row_count * HEAD_SIZE,
        ),
    )(query, keys, values, row_doc, col_doc)


def attention_backward_group(group, query, keys, values, doc_ids, attn, grad, lse, factor):
    row_count = query.shape[0]
    width = GROUP * HEAD_SIZE
    row_doc, col_doc = doc_views(doc_ids)
    flops = 10 * GROUP * row_count * row_count * HEAD_SIZE
    return pl.pallas_call(
        functools.partial(backward_kernel, factor),
        grid=(1,),
        in_specs=[
            pl.BlockSpec((row_count, width), lambda g: (0, group)),
            pl.BlockSpec((row_count, HEAD_SIZE), lambda g: (0, group)),
            pl.BlockSpec((row_count, HEAD_SIZE), lambda g: (0, group)),
            pl.BlockSpec((row_count, 1), lambda g: (0, 0)),
            pl.BlockSpec((1, row_count), lambda g: (0, 0)),
            pl.BlockSpec((row_count, width), lambda g: (0, group)),
            pl.BlockSpec((row_count, width), lambda g: (0, group)),
            pl.BlockSpec((1, GROUP, row_count, HEAD_SIZE), lambda g: (group, 0, 0, 0)),
        ],
        out_specs=[
            pl.BlockSpec((row_count, width), lambda g: (0, 0)),
            pl.BlockSpec((row_count, HEAD_SIZE), lambda g: (0, 0)),
            pl.BlockSpec((row_count, HEAD_SIZE), lambda g: (0, 0)),
        ],
        out_shape=[
            jax.ShapeDtypeStruct((row_count, width), query.dtype),
            jax.ShapeDtypeStruct((row_count, HEAD_SIZE), keys.dtype),
            jax.ShapeDtypeStruct((row_count, HEAD_SIZE), keys.dtype),
        ],
        scratch_shapes=[
            pltpu.VMEM((row_count, HEAD_SIZE), jnp.float32),
            pltpu.VMEM((row_count, HEAD_SIZE), jnp.float32),
        ],
        compiler_params=pltpu.CompilerParams(vmem_limit_bytes=48 * 1024 * 1024),
        cost_estimate=pl.CostEstimate(
            flops=flops // 2, transcendentals=GROUP * row_count * row_count // 2,
            bytes_accessed=2 * 4 * row_count * width + 4 * row_count * HEAD_SIZE * 4
            + 4 * GROUP * row_count * HEAD_SIZE,
        ),
    )(query, keys, values, row_doc, col_doc, attn, grad, lse)


def attach_counts(out_weight, local_counts):
    high = (local_counts // COUNT_BASE).astype(out_weight.dtype)
    low = (local_counts % COUNT_BASE).astype(out_weight.dtype)
    rows = jnp.zeros((16, out_weight.shape[1]), out_weight.dtype)
    rows = rows.at[0, :LANGS].set(high).at[1, :LANGS].set(low)
    return jnp.concatenate([out_weight, rows], axis=0)


def gather_features(block):
    tensor_size = lax.axis_size("tensor")
    me = lax.axis_index("tensor")
    arrived = [block]
    for shift in range(1, tensor_size):
        pairs = [(index, (index + shift) % tensor_size) for index in range(tensor_size)]
        arrived.append(lax.ppermute(block, "tensor", pairs))
    width = block.shape[1]
    full = jnp.zeros((block.shape[0], tensor_size * width), block.dtype)
    for shift, part in enumerate(arrived):
        source = (me - shift) % tensor_size
        full = lax.dynamic_update_slice(full, part, (0, source * width))
    return full


def layer(query, keys, values, out_weight, loss_grad, lengths, languages, labels):
    factor = 1.0 / math.sqrt(HEAD_SIZE)
    row_count = query.shape[0]
    doc_ids = token_docs(lengths[0], row_count).astype(jnp.int32)
    attention_result, log_rows = attention_forward(query, keys, values, doc_ids, factor)
    token_lang = jnp.sum(
        jnp.where(
            doc_ids[:, None] == jnp.arange(DOCS, dtype=jnp.int32)[None, :], languages[0][None, :], 0
        ),
        axis=1,
    )
    counted = labels != -100
    lang_match = token_lang[:, None] == jnp.arange(LANGS, dtype=jnp.int32)[None, :]
    local_counts = jnp.sum((lang_match & counted[:, None]).astype(jnp.int32), axis=0)
    weight_rows = out_weight.shape[0]
    gathered = lax.all_gather(attach_counts(out_weight, local_counts), "dp", axis=1, tiled=True)
    full_weight = gathered[:weight_rows]
    code = gathered[weight_rows : weight_rows + 2].astype(jnp.float32)
    code = code.reshape(2, lax.axis_size("dp"), out_weight.shape[1])[:, :, :LANGS]
    counts = jnp.sum(code[0] * COUNT_BASE + code[1], axis=0)
    lang_weight = jnp.sqrt(jnp.sum(counts) / (LANGS * jnp.maximum(counts, 1.0)))
    token_weight = jnp.where(
        counted, jnp.sum(jnp.where(lang_match, lang_weight[None, :], 0.0), axis=1), 0.0
    )
    full_grad = gather_features(loss_grad)
    weighted = (token_weight[:, None] * full_grad.astype(jnp.float32)).astype(jnp.bfloat16)
    local_term = lax.dot_general(
        attention_result, weighted, (((0,), (0,)), ((), ())), preferred_element_type=jnp.float32
    )
    projection_part = lax.psum_scatter(
        local_term.astype(jnp.bfloat16), "dp", scatter_dimension=0, tiled=True
    )
    projection_gradient = lax.all_gather(projection_part, "dp", axis=0, tiled=True)
    local_term, weighted = lax.optimization_barrier((local_term, weighted))
    out_grad = lax.dot_general(
        weighted,
        full_weight,
        (((1,), (1,)), ((), ())),
        preferred_element_type=jnp.float32,
    ).astype(jnp.bfloat16)

    parts = []
    for group in range(keys.shape[1] // HEAD_SIZE):
        parts.append(
            attention_backward_group(
                group, query, keys, values, doc_ids, attention_result, out_grad, log_rows, factor
            )
        )
    query_gradient, key_gradient, value_gradient = (
        jnp.concatenate([part[k] for part in parts], axis=1) for k in range(3)
    )
    return (attention_result, query_gradient, key_gradient, value_gradient, projection_gradient)


def solution(mesh):
    in_specs = (
        P("dp", "tensor"),
        P("dp", "tensor"),
        P("dp", "tensor"),
        P("tensor", "dp"),
        P("dp", "tensor"),
        P("dp", None),
        P("dp", None),
        P("dp"),
    )
    out_specs = (
        P("dp", "tensor"),
        P("dp", "tensor"),
        P("dp", "tensor"),
        P("dp", "tensor"),
        P("tensor", None),
    )
    return jax.shard_map(layer, mesh=mesh, in_specs=in_specs, out_specs=out_specs, check_vma=False)
```

```python
import functools
import math

import jax
import jax.numpy as jnp
from jax import lax
from jax.experimental import pallas as pl
from jax.experimental.pallas import tpu as pltpu
from jax.sharding import PartitionSpec as P


QUERY_HEADS = 40
KEY_VALUE_HEADS = 8
HEAD_SIZE = 128
LANGS = 29
DOCS = 16
COUNT_BASE = 32


def token_docs(length_row, row_count):
    doc_ends = jnp.cumsum(length_row)
    places = jnp.arange(row_count, dtype=jnp.int32)
    return jnp.sum((places[:, None] >= doc_ends[None, :]).astype(jnp.int32), axis=1)


GROUP = QUERY_HEADS // KEY_VALUE_HEADS
ROW_BLOCK = 256
MASKED = -1e30
NT_DIMS = (((1,), (1,)), ((), ()))


def block_mask(row_doc_ref, col_doc_ref, first_row, key_end):
    row_doc = row_doc_ref[first_row : first_row + ROW_BLOCK, :]
    col_doc = col_doc_ref[:, :key_end]
    shape = (ROW_BLOCK, key_end)
    rows = lax.broadcasted_iota(jnp.int32, shape, 0) + first_row
    cols = lax.broadcasted_iota(jnp.int32, shape, 1)
    return (row_doc == col_doc) & (cols <= rows)


def forward_kernel(factor, q_ref, k_ref, v_ref, row_doc_ref, col_doc_ref, o_ref, lse_ref):
    row_count = q_ref.shape[0]
    for block in range(row_count // ROW_BLOCK):
        first_row = block * ROW_BLOCK
        key_end = first_row + ROW_BLOCK
        allowed = block_mask(row_doc_ref, col_doc_ref, first_row, key_end)
        rows = pl.ds(first_row, ROW_BLOCK)

        def head_body(head, carry):
            cols = pl.ds(pl.multiple_of(head * HEAD_SIZE, HEAD_SIZE), HEAD_SIZE)
            query = q_ref[rows, cols]
            scores = lax.dot_general(
                query, k_ref[:key_end, :], NT_DIMS, preferred_element_type=jnp.float32
            ) * factor
            scores = jnp.where(allowed, scores, MASKED)
            top = jnp.max(scores, axis=1, keepdims=True)
            log_total = top + jnp.log(jnp.sum(jnp.exp(scores - top), axis=1, keepdims=True))
            weights = jnp.exp(scores - log_total).astype(jnp.bfloat16)
            result = jnp.dot(weights, v_ref[:key_end, :], preferred_element_type=jnp.float32)
            o_ref[rows, cols] = result.astype(o_ref.dtype)
            lse_ref[0, head, rows, :] = jnp.broadcast_to(log_total, (ROW_BLOCK, HEAD_SIZE))
            return carry

        lax.fori_loop(0, GROUP, head_body, 0)


def backward_kernel(
    factor, q_ref, k_ref, v_ref, row_doc_ref, col_doc_ref, o_ref, do_ref, lse_ref,
    dq_ref, dk_ref, dv_ref, dk_acc, dv_acc,
):
    row_count = q_ref.shape[0]
    dk_acc[...] = jnp.zeros_like(dk_acc)
    dv_acc[...] = jnp.zeros_like(dv_acc)
    for block in range(row_count // ROW_BLOCK):
        first_row = block * ROW_BLOCK
        key_end = first_row + ROW_BLOCK
        allowed = block_mask(row_doc_ref, col_doc_ref, first_row, key_end)
        rows = pl.ds(first_row, ROW_BLOCK)

        def head_body(head, carry):
            cols = pl.ds(pl.multiple_of(head * HEAD_SIZE, HEAD_SIZE), HEAD_SIZE)
            query = q_ref[rows, cols]
            grad = do_ref[rows, cols]
            keys = k_ref[:key_end, :]
            values = v_ref[:key_end, :]
            log_total = lse_ref[0, head, rows, :][:, :1]
            scores = lax.dot_general(query, keys, NT_DIMS, preferred_element_type=jnp.float32) * factor
            scores = jnp.where(allowed, scores, MASKED)
            weights = jnp.exp(scores - log_total)
            dv_acc[:key_end, :] += jnp.dot(
                weights.astype(jnp.bfloat16).T, grad, preferred_element_type=jnp.float32
            )
            weight_grad = lax.dot_general(grad, values, NT_DIMS, preferred_element_type=jnp.float32)
            diagonal = jnp.sum(
                grad.astype(jnp.float32) * o_ref[rows, cols].astype(jnp.float32), axis=1, keepdims=True
            )
            score_grad = (weights * (weight_grad - diagonal) * factor).astype(jnp.bfloat16)
            dq_ref[rows, cols] = jnp.dot(score_grad, keys, preferred_element_type=jnp.float32).astype(
                dq_ref.dtype
            )
            dk_acc[:key_end, :] += jnp.dot(score_grad.T, query, preferred_element_type=jnp.float32)
            return carry

        lax.fori_loop(0, GROUP, head_body, 0)
    dk_ref[...] = dk_acc[...].astype(dk_ref.dtype)
    dv_ref[...] = dv_acc[...].astype(dv_ref.dtype)


def doc_views(doc_ids):
    return doc_ids[:, None], doc_ids[None, :]


def attention_forward(query, keys, values, doc_ids, factor):
    row_count = query.shape[0]
    groups = keys.shape[1] // HEAD_SIZE
    width = GROUP * HEAD_SIZE
    row_doc, col_doc = doc_views(doc_ids)
    flops = 4 * groups * GROUP * row_count * row_count * HEAD_SIZE
    return pl.pallas_call(
        functools.partial(forward_kernel, factor),
        grid=(groups,),
        in_specs=[
            pl.BlockSpec((row_count, width), lambda g: (0, g)),
            pl.BlockSpec((row_count, HEAD_SIZE), lambda g: (0, g)),
            pl.BlockSpec((row_count, HEAD_SIZE), lambda g: (0, g)),
            pl.BlockSpec((row_count, 1), lambda g: (0, 0)),
            pl.BlockSpec((1, row_count), lambda g: (0, 0)),
        ],
        out_specs=[
            pl.BlockSpec((row_count, width), lambda g: (0, g)),
            pl.BlockSpec((1, GROUP, row_count, HEAD_SIZE), lambda g: (g, 0, 0, 0)),
        ],
        out_shape=[
            jax.ShapeDtypeStruct(query.shape, query.dtype),
            jax.ShapeDtypeStruct((groups, GROUP, row_count, HEAD_SIZE), jnp.float32),
        ],
        compiler_params=pltpu.CompilerParams(vmem_limit_bytes=48 * 1024 * 1024),
        cost_estimate=pl.CostEstimate(
            flops=flops // 2, transcendentals=groups * GROUP * row_count * row_count // 2,
            bytes_accessed=4 * query.size + 8 * keys.size + 8 * groups * GROUP * row_count * HEAD_SIZE,
        ),
    )(query, keys, values, row_doc, col_doc)


def attention_backward_group(group, query, keys, values, doc_ids, attn, grad, lse, factor):
    row_count = query.shape[0]
    width = GROUP * HEAD_SIZE
    row_doc, col_doc = doc_views(doc_ids)
    flops = 10 * GROUP * row_count * row_count * HEAD_SIZE
    return pl.pallas_call(
        functools.partial(backward_kernel, factor),
        grid=(1,),
        in_specs=[
            pl.BlockSpec((row_count, width), lambda g: (0, group)),
            pl.BlockSpec((row_count, HEAD_SIZE), lambda g: (0, group)),
            pl.BlockSpec((row_count, HEAD_SIZE), lambda g: (0, group)),
            pl.BlockSpec((row_count, 1), lambda g: (0, 0)),
            pl.BlockSpec((1, row_count), lambda g: (0, 0)),
            pl.BlockSpec((row_count, width), lambda g: (0, group)),
            pl.BlockSpec((row_count, width), lambda g: (0, group)),
            pl.BlockSpec((1, GROUP, row_count, HEAD_SIZE), lambda g: (group, 0, 0, 0)),
        ],
        out_specs=[
            pl.BlockSpec((row_count, width), lambda g: (0, 0)),
            pl.BlockSpec((row_count, HEAD_SIZE), lambda g: (0, 0)),
            pl.BlockSpec((row_count, HEAD_SIZE), lambda g: (0, 0)),
        ],
        out_shape=[
            jax.ShapeDtypeStruct((row_count, width), query.dtype),
            jax.ShapeDtypeStruct((row_count, HEAD_SIZE), keys.dtype),
            jax.ShapeDtypeStruct((row_count, HEAD_SIZE), keys.dtype),
        ],
        scratch_shapes=[
            pltpu.VMEM((row_count, HEAD_SIZE), jnp.float32),
            pltpu.VMEM((row_count, HEAD_SIZE), jnp.float32),
        ],
        compiler_params=pltpu.CompilerParams(vmem_limit_bytes=48 * 1024 * 1024),
        cost_estimate=pl.CostEstimate(
            flops=flops // 2, transcendentals=GROUP * row_count * row_count // 2,
            bytes_accessed=2 * 4 * row_count * width + 4 * row_count * HEAD_SIZE * 4
            + 4 * GROUP * row_count * HEAD_SIZE,
        ),
    )(query, keys, values, row_doc, col_doc, attn, grad, lse)


def attach_counts(out_weight, local_counts):
    high = (local_counts // COUNT_BASE).astype(out_weight.dtype)
    low = (local_counts % COUNT_BASE).astype(out_weight.dtype)
    rows = jnp.zeros((16, out_weight.shape[1]), out_weight.dtype)
    rows = rows.at[0, :LANGS].set(high).at[1, :LANGS].set(low)
    return jnp.concatenate([out_weight, rows], axis=0)


def gather_features(block):
    tensor_size = lax.axis_size("tensor")
    me = lax.axis_index("tensor")
    arrived = [(me, block)]
    for shift in range(1, tensor_size):
        pairs = [(index, (index + shift) % tensor_size) for index in range(tensor_size)]
        moved = lax.ppermute(block, "tensor", pairs)
        arrived.append(((me - shift) % tensor_size, moved))
    return arrived


def place_blocks(blocks, width):
    full = jnp.zeros((blocks[0][1].shape[0], len(blocks) * width), blocks[0][1].dtype)
    for source, part in blocks:
        full = lax.dynamic_update_slice(full, part, (0, source * width))
    return full


def layer(query, keys, values, out_weight, loss_grad, lengths, languages, labels):
    factor = 1.0 / math.sqrt(HEAD_SIZE)
    row_count = query.shape[0]
    doc_ids = token_docs(lengths[0], row_count).astype(jnp.int32)
    attention_result, log_rows = attention_forward(query, keys, values, doc_ids, factor)
    token_lang = jnp.sum(
        jnp.where(
            doc_ids[:, None] == jnp.arange(DOCS, dtype=jnp.int32)[None, :], languages[0][None, :], 0
        ),
        axis=1,
    )
    counted = labels != -100
    lang_match = token_lang[:, None] == jnp.arange(LANGS, dtype=jnp.int32)[None, :]
    local_counts = jnp.sum((lang_match & counted[:, None]).astype(jnp.int32), axis=0)
    weight_rows = out_weight.shape[0]
    gathered = lax.all_gather(attach_counts(out_weight, local_counts), "dp", axis=1, tiled=True)
    full_weight = gathered[:weight_rows]
    code = gathered[weight_rows : weight_rows + 2].astype(jnp.float32)
    code = code.reshape(2, lax.axis_size("dp"), out_weight.shape[1])[:, :, :LANGS]
    counts = jnp.sum(code[0] * COUNT_BASE + code[1], axis=0)
    lang_weight = jnp.sqrt(jnp.sum(counts) / (LANGS * jnp.maximum(counts, 1.0)))
    token_weight = jnp.where(
        counted, jnp.sum(jnp.where(lang_match, lang_weight[None, :], 0.0), axis=1), 0.0
    )
    width = loss_grad.shape[1]
    weighted_blocks = [
        (source, (token_weight[:, None] * part.astype(jnp.float32)).astype(jnp.bfloat16))
        for source, part in gather_features(loss_grad)
    ]
    scattered = []
    for source, part in weighted_blocks:
        local_term = lax.dot_general(
            attention_result, part, (((0,), (0,)), ((), ())), preferred_element_type=jnp.float32
        )
        scattered.append(
            (
                source,
                lax.psum_scatter(
                    local_term.astype(jnp.bfloat16), "dp", scatter_dimension=0, tiled=True
                ),
            )
        )
    projection_gradient = lax.all_gather(place_blocks(scattered, width), "dp", axis=0, tiled=True)
    weighted = place_blocks(weighted_blocks, width)
    out_grad = lax.dot_general(
        weighted,
        full_weight,
        (((1,), (1,)), ((), ())),
        preferred_element_type=jnp.float32,
    ).astype(jnp.bfloat16)

    parts = []
    for group in range(keys.shape[1] // HEAD_SIZE):
        parts.append(
            attention_backward_group(
                group, query, keys, values, doc_ids, attention_result, out_grad, log_rows, factor
            )
        )
    query_gradient, key_gradient, value_gradient = (
        jnp.concatenate([part[k] for part in parts], axis=1) for k in range(3)
    )
    return (attention_result, query_gradient, key_gradient, value_gradient, projection_gradient)


def solution(mesh):
    in_specs = (
        P("dp", "tensor"),
        P("dp", "tensor"),
        P("dp", "tensor"),
        P("tensor", "dp"),
        P("dp", "tensor"),
        P("dp", None),
        P("dp", None),
        P("dp"),
    )
    out_specs = (
        P("dp", "tensor"),
        P("dp", "tensor"),
        P("dp", "tensor"),
        P("dp", "tensor"),
        P("tensor", None),
    )
    return jax.shard_map(layer, mesh=mesh, in_specs=in_specs, out_specs=out_specs, check_vma=False)
```

```python
import functools
import math

import jax
import jax.numpy as jnp
from jax import lax
from jax.experimental import pallas as pl
from jax.experimental.pallas import tpu as pltpu
from jax.sharding import PartitionSpec as P


QUERY_HEADS = 40
KEY_VALUE_HEADS = 8
HEAD_SIZE = 128
LANGS = 29
DOCS = 16
COUNT_BASE = 32
DP_AXES = ("dp_x", "dp_y", "dp_core")


def token_docs(length_row, row_count):
    doc_ends = jnp.cumsum(length_row)
    places = jnp.arange(row_count, dtype=jnp.int32)
    return jnp.sum((places[:, None] >= doc_ends[None, :]).astype(jnp.int32), axis=1)


GROUP = QUERY_HEADS // KEY_VALUE_HEADS
ROW_BLOCK = 256
MASKED = -1e30
NT_DIMS = (((1,), (1,)), ((), ()))


def block_mask(row_doc_ref, col_doc_ref, first_row, key_end):
    row_doc = row_doc_ref[first_row : first_row + ROW_BLOCK, :]
    col_doc = col_doc_ref[:, :key_end]
    shape = (ROW_BLOCK, key_end)
    rows = lax.broadcasted_iota(jnp.int32, shape, 0) + first_row
    cols = lax.broadcasted_iota(jnp.int32, shape, 1)
    return (row_doc == col_doc) & (cols <= rows)


def forward_kernel(factor, q_ref, k_ref, v_ref, row_doc_ref, col_doc_ref, o_ref, lse_ref):
    row_count = q_ref.shape[0]
    for block in range(row_count // ROW_BLOCK):
        first_row = block * ROW_BLOCK
        key_end = first_row + ROW_BLOCK
        allowed = block_mask(row_doc_ref, col_doc_ref, first_row, key_end)
        rows = pl.ds(first_row, ROW_BLOCK)

        def head_body(head, carry):
            cols = pl.ds(pl.multiple_of(head * HEAD_SIZE, HEAD_SIZE), HEAD_SIZE)
            query = q_ref[rows, cols]
            scores = lax.dot_general(
                query, k_ref[:key_end, :], NT_DIMS, preferred_element_type=jnp.float32
            ) * factor
            scores = jnp.where(allowed, scores, MASKED)
            top = jnp.max(scores, axis=1, keepdims=True)
            log_total = top + jnp.log(jnp.sum(jnp.exp(scores - top), axis=1, keepdims=True))
            weights = jnp.exp(scores - log_total).astype(jnp.bfloat16)
            result = jnp.dot(weights, v_ref[:key_end, :], preferred_element_type=jnp.float32)
            o_ref[rows, cols] = result.astype(o_ref.dtype)
            lse_ref[0, head, rows, :] = jnp.broadcast_to(log_total, (ROW_BLOCK, HEAD_SIZE))
            return carry

        lax.fori_loop(0, GROUP, head_body, 0)


def backward_kernel(
    factor, q_ref, k_ref, v_ref, row_doc_ref, col_doc_ref, o_ref, do_ref, lse_ref,
    dq_ref, dk_ref, dv_ref, dk_acc, dv_acc,
):
    row_count = q_ref.shape[0]
    dk_acc[...] = jnp.zeros_like(dk_acc)
    dv_acc[...] = jnp.zeros_like(dv_acc)
    for block in range(row_count // ROW_BLOCK):
        first_row = block * ROW_BLOCK
        key_end = first_row + ROW_BLOCK
        allowed = block_mask(row_doc_ref, col_doc_ref, first_row, key_end)
        rows = pl.ds(first_row, ROW_BLOCK)

        def head_body(head, carry):
            cols = pl.ds(pl.multiple_of(head * HEAD_SIZE, HEAD_SIZE), HEAD_SIZE)
            query = q_ref[rows, cols]
            grad = do_ref[rows, cols]
            keys = k_ref[:key_end, :]
            values = v_ref[:key_end, :]
            log_total = lse_ref[0, head, rows, :][:, :1]
            scores = lax.dot_general(query, keys, NT_DIMS, preferred_element_type=jnp.float32) * factor
            scores = jnp.where(allowed, scores, MASKED)
            weights = jnp.exp(scores - log_total)
            dv_acc[:key_end, :] += jnp.dot(
                weights.astype(jnp.bfloat16).T, grad, preferred_element_type=jnp.float32
            )
            weight_grad = lax.dot_general(grad, values, NT_DIMS, preferred_element_type=jnp.float32)
            diagonal = jnp.sum(
                grad.astype(jnp.float32) * o_ref[rows, cols].astype(jnp.float32), axis=1, keepdims=True
            )
            score_grad = (weights * (weight_grad - diagonal) * factor).astype(jnp.bfloat16)
            dq_ref[rows, cols] = jnp.dot(score_grad, keys, preferred_element_type=jnp.float32).astype(
                dq_ref.dtype
            )
            dk_acc[:key_end, :] += jnp.dot(score_grad.T, query, preferred_element_type=jnp.float32)
            return carry

        lax.fori_loop(0, GROUP, head_body, 0)
    dk_ref[...] = dk_acc[...].astype(dk_ref.dtype)
    dv_ref[...] = dv_acc[...].astype(dv_ref.dtype)


def doc_views(doc_ids):
    return doc_ids[:, None], doc_ids[None, :]


def attention_forward(query, keys, values, doc_ids, factor):
    row_count = query.shape[0]
    groups = keys.shape[1] // HEAD_SIZE
    width = GROUP * HEAD_SIZE
    row_doc, col_doc = doc_views(doc_ids)
    flops = 4 * groups * GROUP * row_count * row_count * HEAD_SIZE
    return pl.pallas_call(
        functools.partial(forward_kernel, factor),
        grid=(groups,),
        in_specs=[
            pl.BlockSpec((row_count, width), lambda g: (0, g)),
            pl.BlockSpec((row_count, HEAD_SIZE), lambda g: (0, g)),
            pl.BlockSpec((row_count, HEAD_SIZE), lambda g: (0, g)),
            pl.BlockSpec((row_count, 1), lambda g: (0, 0)),
            pl.BlockSpec((1, row_count), lambda g: (0, 0)),
        ],
        out_specs=[
            pl.BlockSpec((row_count, width), lambda g: (0, g)),
            pl.BlockSpec((1, GROUP, row_count, HEAD_SIZE), lambda g: (g, 0, 0, 0)),
        ],
        out_shape=[
            jax.ShapeDtypeStruct(query.shape, query.dtype),
            jax.ShapeDtypeStruct((groups, GROUP, row_count, HEAD_SIZE), jnp.float32),
        ],
        compiler_params=pltpu.CompilerParams(vmem_limit_bytes=48 * 1024 * 1024),
        cost_estimate=pl.CostEstimate(
            flops=flops // 2, transcendentals=groups * GROUP * row_count * row_count // 2,
            bytes_accessed=4 * query.size + 8 * keys.size + 8 * groups * GROUP * row_count * HEAD_SIZE,
        ),
    )(query, keys, values, row_doc, col_doc)


def attention_backward_group(group, query, keys, values, doc_ids, attn, grad, lse, factor):
    row_count = query.shape[0]
    width = GROUP * HEAD_SIZE
    row_doc, col_doc = doc_views(doc_ids)
    flops = 10 * GROUP * row_count * row_count * HEAD_SIZE
    return pl.pallas_call(
        functools.partial(backward_kernel, factor),
        grid=(1,),
        in_specs=[
            pl.BlockSpec((row_count, width), lambda g: (0, group)),
            pl.BlockSpec((row_count, HEAD_SIZE), lambda g: (0, group)),
            pl.BlockSpec((row_count, HEAD_SIZE), lambda g: (0, group)),
            pl.BlockSpec((row_count, 1), lambda g: (0, 0)),
            pl.BlockSpec((1, row_count), lambda g: (0, 0)),
            pl.BlockSpec((row_count, width), lambda g: (0, group)),
            pl.BlockSpec((row_count, width), lambda g: (0, group)),
            pl.BlockSpec((1, GROUP, row_count, HEAD_SIZE), lambda g: (group, 0, 0, 0)),
        ],
        out_specs=[
            pl.BlockSpec((row_count, width), lambda g: (0, 0)),
            pl.BlockSpec((row_count, HEAD_SIZE), lambda g: (0, 0)),
            pl.BlockSpec((row_count, HEAD_SIZE), lambda g: (0, 0)),
        ],
        out_shape=[
            jax.ShapeDtypeStruct((row_count, width), query.dtype),
            jax.ShapeDtypeStruct((row_count, HEAD_SIZE), keys.dtype),
            jax.ShapeDtypeStruct((row_count, HEAD_SIZE), keys.dtype),
        ],
        scratch_shapes=[
            pltpu.VMEM((row_count, HEAD_SIZE), jnp.float32),
            pltpu.VMEM((row_count, HEAD_SIZE), jnp.float32),
        ],
        compiler_params=pltpu.CompilerParams(vmem_limit_bytes=48 * 1024 * 1024),
        cost_estimate=pl.CostEstimate(
            flops=flops // 2, transcendentals=GROUP * row_count * row_count // 2,
            bytes_accessed=2 * 4 * row_count * width + 4 * row_count * HEAD_SIZE * 4
            + 4 * GROUP * row_count * HEAD_SIZE,
        ),
    )(query, keys, values, row_doc, col_doc, attn, grad, lse)


def attach_counts(out_weight, local_counts):
    high = (local_counts // COUNT_BASE).astype(out_weight.dtype)
    low = (local_counts % COUNT_BASE).astype(out_weight.dtype)
    rows = jnp.zeros((16, out_weight.shape[1]), out_weight.dtype)
    rows = rows.at[0, :LANGS].set(high).at[1, :LANGS].set(low)
    return jnp.concatenate([out_weight, rows], axis=0)


def gather_features(block):
    tensor_size = lax.axis_size("tensor")
    me = lax.axis_index("tensor")
    arrived = [block]
    for shift in range(1, tensor_size):
        pairs = [(index, (index + shift) % tensor_size) for index in range(tensor_size)]
        arrived.append(lax.ppermute(block, "tensor", pairs))
    width = block.shape[1]
    full = jnp.zeros((block.shape[0], tensor_size * width), block.dtype)
    for shift, part in enumerate(arrived):
        source = (me - shift) % tensor_size
        full = lax.dynamic_update_slice(full, part, (0, source * width))
    return full


def layer(query, keys, values, out_weight, loss_grad, lengths, languages, labels):
    factor = 1.0 / math.sqrt(HEAD_SIZE)
    row_count = query.shape[0]
    doc_ids = token_docs(lengths[0], row_count).astype(jnp.int32)
    attention_result, log_rows = attention_forward(query, keys, values, doc_ids, factor)
    token_lang = jnp.sum(
        jnp.where(
            doc_ids[:, None] == jnp.arange(DOCS, dtype=jnp.int32)[None, :], languages[0][None, :], 0
        ),
        axis=1,
    )
    counted = labels != -100
    lang_match = token_lang[:, None] == jnp.arange(LANGS, dtype=jnp.int32)[None, :]
    local_counts = jnp.sum((lang_match & counted[:, None]).astype(jnp.int32), axis=0)
    weight_rows = out_weight.shape[0]
    gathered = lax.all_gather(attach_counts(out_weight, local_counts), DP_AXES, axis=1, tiled=True)
    full_weight = gathered[:weight_rows]
    code = gathered[weight_rows : weight_rows + 2].astype(jnp.float32)
    code = code.reshape(2, lax.axis_size(DP_AXES), out_weight.shape[1])[:, :, :LANGS]
    counts = jnp.sum(code[0] * COUNT_BASE + code[1], axis=0)
    lang_weight = jnp.sqrt(jnp.sum(counts) / (LANGS * jnp.maximum(counts, 1.0)))
    token_weight = jnp.where(
        counted, jnp.sum(jnp.where(lang_match, lang_weight[None, :], 0.0), axis=1), 0.0
    )
    full_grad = gather_features(loss_grad)
    weighted = (token_weight[:, None] * full_grad.astype(jnp.float32)).astype(jnp.bfloat16)
    local_term = lax.dot_general(
        attention_result, weighted, (((0,), (0,)), ((), ())), preferred_element_type=jnp.float32
    )
    projection_part = local_term.astype(jnp.bfloat16)
    for axis in reversed(DP_AXES):
        projection_part = lax.psum_scatter(
            projection_part, axis, scatter_dimension=0, tiled=True
        )
    projection_gradient = projection_part
    for axis in DP_AXES:
        projection_gradient = lax.all_gather(projection_gradient, axis, axis=0, tiled=True)
    local_term, weighted = lax.optimization_barrier((local_term, weighted))
    out_grad = lax.dot_general(
        weighted,
        full_weight,
        (((1,), (1,)), ((), ())),
        preferred_element_type=jnp.float32,
    ).astype(jnp.bfloat16)

    parts = []
    for group in range(keys.shape[1] // HEAD_SIZE):
        parts.append(
            attention_backward_group(group, query, keys, values, doc_ids, attention_result, out_grad, log_rows, factor)
        )
    query_gradient, key_gradient, value_gradient = (
        jnp.concatenate([part[k] for part in parts], axis=1) for k in range(3)
    )
    return (attention_result, query_gradient, key_gradient, value_gradient, projection_gradient)


def solution(mesh):
    in_specs = (
        P(DP_AXES, "tensor"),
        P(DP_AXES, "tensor"),
        P(DP_AXES, "tensor"),
        P("tensor", DP_AXES),
        P(DP_AXES, "tensor"),
        P(DP_AXES, None),
        P(DP_AXES, None),
        P(DP_AXES),
    )
    out_specs = (
        P(DP_AXES, "tensor"),
        P(DP_AXES, "tensor"),
        P(DP_AXES, "tensor"),
        P(DP_AXES, "tensor"),
        P("tensor", None),
    )
    dp = mesh.shape["dp"]
    split_mesh = jax.sharding.Mesh(
        mesh.devices.reshape(dp // 8, 4, 2, mesh.shape["tensor"]), DP_AXES + ("tensor",)
    )
    return jax.shard_map(layer, mesh=split_mesh, in_specs=in_specs, out_specs=out_specs, check_vma=False)
```

```python
import functools
import math

import jax
import jax.numpy as jnp
from jax import lax
from jax.experimental import pallas as pl
from jax.experimental.pallas import tpu as pltpu
from jax.sharding import PartitionSpec as P


QUERY_HEADS = 40
KEY_VALUE_HEADS = 8
HEAD_SIZE = 128
LANGS = 29
DOCS = 16
COUNT_BASE = 32


def token_docs(length_row, row_count):
    doc_ends = jnp.cumsum(length_row)
    places = jnp.arange(row_count, dtype=jnp.int32)
    return jnp.sum((places[:, None] >= doc_ends[None, :]).astype(jnp.int32), axis=1)


GROUP = QUERY_HEADS // KEY_VALUE_HEADS
ROW_BLOCK = 256
MASKED = -1e30
NT_DIMS = (((1,), (1,)), ((), ()))


def block_mask(row_doc_ref, col_doc_ref, first_row, key_end):
    row_doc = row_doc_ref[first_row : first_row + ROW_BLOCK, :]
    col_doc = col_doc_ref[:, :key_end]
    shape = (ROW_BLOCK, key_end)
    rows = lax.broadcasted_iota(jnp.int32, shape, 0) + first_row
    cols = lax.broadcasted_iota(jnp.int32, shape, 1)
    return (row_doc == col_doc) & (cols <= rows)


def forward_kernel(factor, q_ref, k_ref, v_ref, row_doc_ref, col_doc_ref, o_ref, lse_ref):
    row_count = q_ref.shape[0]
    for block in range(row_count // ROW_BLOCK):
        first_row = block * ROW_BLOCK
        key_end = first_row + ROW_BLOCK
        allowed = block_mask(row_doc_ref, col_doc_ref, first_row, key_end)
        rows = pl.ds(first_row, ROW_BLOCK)

        def head_body(head, carry):
            cols = pl.ds(pl.multiple_of(head * HEAD_SIZE, HEAD_SIZE), HEAD_SIZE)
            query = q_ref[rows, cols]
            scores = lax.dot_general(
                query, k_ref[:key_end, :], NT_DIMS, preferred_element_type=jnp.float32
            ) * factor
            scores = jnp.where(allowed, scores, MASKED)
            top = jnp.max(scores, axis=1, keepdims=True)
            log_total = top + jnp.log(jnp.sum(jnp.exp(scores - top), axis=1, keepdims=True))
            weights = jnp.exp(scores - log_total).astype(jnp.bfloat16)
            result = jnp.dot(weights, v_ref[:key_end, :], preferred_element_type=jnp.float32)
            o_ref[rows, cols] = result.astype(o_ref.dtype)
            lse_ref[0, head, rows, :] = jnp.broadcast_to(log_total, (ROW_BLOCK, HEAD_SIZE))
            return carry

        lax.fori_loop(0, GROUP, head_body, 0)


def backward_kernel(
    factor, q_ref, k_ref, v_ref, row_doc_ref, col_doc_ref, o_ref, do_ref, lse_ref,
    dq_ref, dk_ref, dv_ref, dk_acc, dv_acc,
):
    row_count = q_ref.shape[0]
    dk_acc[...] = jnp.zeros_like(dk_acc)
    dv_acc[...] = jnp.zeros_like(dv_acc)
    for block in range(row_count // ROW_BLOCK):
        first_row = block * ROW_BLOCK
        key_end = first_row + ROW_BLOCK
        allowed = block_mask(row_doc_ref, col_doc_ref, first_row, key_end)
        rows = pl.ds(first_row, ROW_BLOCK)

        def head_body(head, carry):
            cols = pl.ds(pl.multiple_of(head * HEAD_SIZE, HEAD_SIZE), HEAD_SIZE)
            query = q_ref[rows, cols]
            grad = do_ref[rows, cols]
            keys = k_ref[:key_end, :]
            values = v_ref[:key_end, :]
            log_total = lse_ref[0, head, rows, :][:, :1]
            scores = lax.dot_general(query, keys, NT_DIMS, preferred_element_type=jnp.float32) * factor
            scores = jnp.where(allowed, scores, MASKED)
            weights = jnp.exp(scores - log_total)
            dv_acc[:key_end, :] += jnp.dot(
                weights.astype(jnp.bfloat16).T, grad, preferred_element_type=jnp.float32
            )
            weight_grad = lax.dot_general(grad, values, NT_DIMS, preferred_element_type=jnp.float32)
            diagonal = jnp.sum(
                grad.astype(jnp.float32) * o_ref[rows, cols].astype(jnp.float32), axis=1, keepdims=True
            )
            score_grad = (weights * (weight_grad - diagonal) * factor).astype(jnp.bfloat16)
            dq_ref[rows, cols] = jnp.dot(score_grad, keys, preferred_element_type=jnp.float32).astype(
                dq_ref.dtype
            )
            dk_acc[:key_end, :] += jnp.dot(score_grad.T, query, preferred_element_type=jnp.float32)
            return carry

        lax.fori_loop(0, GROUP, head_body, 0)
    dk_ref[...] = dk_acc[...].astype(dk_ref.dtype)
    dv_ref[...] = dv_acc[...].astype(dv_ref.dtype)


def doc_views(doc_ids):
    return doc_ids[:, None], doc_ids[None, :]


def attention_forward(query, keys, values, doc_ids, factor):
    row_count = query.shape[0]
    groups = keys.shape[1] // HEAD_SIZE
    width = GROUP * HEAD_SIZE
    row_doc, col_doc = doc_views(doc_ids)
    flops = 4 * groups * GROUP * row_count * row_count * HEAD_SIZE
    return pl.pallas_call(
        functools.partial(forward_kernel, factor),
        grid=(groups,),
        in_specs=[
            pl.BlockSpec((row_count, width), lambda g: (0, g)),
            pl.BlockSpec((row_count, HEAD_SIZE), lambda g: (0, g)),
            pl.BlockSpec((row_count, HEAD_SIZE), lambda g: (0, g)),
            pl.BlockSpec((row_count, 1), lambda g: (0, 0)),
            pl.BlockSpec((1, row_count), lambda g: (0, 0)),
        ],
        out_specs=[
            pl.BlockSpec((row_count, width), lambda g: (0, g)),
            pl.BlockSpec((1, GROUP, row_count, HEAD_SIZE), lambda g: (g, 0, 0, 0)),
        ],
        out_shape=[
            jax.ShapeDtypeStruct(query.shape, query.dtype),
            jax.ShapeDtypeStruct((groups, GROUP, row_count, HEAD_SIZE), jnp.float32),
        ],
        compiler_params=pltpu.CompilerParams(vmem_limit_bytes=48 * 1024 * 1024),
        cost_estimate=pl.CostEstimate(
            flops=flops // 2, transcendentals=groups * GROUP * row_count * row_count // 2,
            bytes_accessed=4 * query.size + 8 * keys.size + 8 * groups * GROUP * row_count * HEAD_SIZE,
        ),
    )(query, keys, values, row_doc, col_doc)


def attention_backward_group(group, query, keys, values, doc_ids, attn, grad, lse, factor):
    row_count = query.shape[0]
    width = GROUP * HEAD_SIZE
    row_doc, col_doc = doc_views(doc_ids)
    flops = 10 * GROUP * row_count * row_count * HEAD_SIZE
    return pl.pallas_call(
        functools.partial(backward_kernel, factor),
        grid=(1,),
        in_specs=[
            pl.BlockSpec((row_count, width), lambda g: (0, group)),
            pl.BlockSpec((row_count, HEAD_SIZE), lambda g: (0, group)),
            pl.BlockSpec((row_count, HEAD_SIZE), lambda g: (0, group)),
            pl.BlockSpec((row_count, 1), lambda g: (0, 0)),
            pl.BlockSpec((1, row_count), lambda g: (0, 0)),
            pl.BlockSpec((row_count, width), lambda g: (0, group)),
            pl.BlockSpec((row_count, width), lambda g: (0, group)),
            pl.BlockSpec((1, GROUP, row_count, HEAD_SIZE), lambda g: (group, 0, 0, 0)),
        ],
        out_specs=[
            pl.BlockSpec((row_count, width), lambda g: (0, 0)),
            pl.BlockSpec((row_count, HEAD_SIZE), lambda g: (0, 0)),
            pl.BlockSpec((row_count, HEAD_SIZE), lambda g: (0, 0)),
        ],
        out_shape=[
            jax.ShapeDtypeStruct((row_count, width), query.dtype),
            jax.ShapeDtypeStruct((row_count, HEAD_SIZE), keys.dtype),
            jax.ShapeDtypeStruct((row_count, HEAD_SIZE), keys.dtype),
        ],
        scratch_shapes=[
            pltpu.VMEM((row_count, HEAD_SIZE), jnp.float32),
            pltpu.VMEM((row_count, HEAD_SIZE), jnp.float32),
        ],
        compiler_params=pltpu.CompilerParams(vmem_limit_bytes=48 * 1024 * 1024),
        cost_estimate=pl.CostEstimate(
            flops=flops // 2, transcendentals=GROUP * row_count * row_count // 2,
            bytes_accessed=2 * 4 * row_count * width + 4 * row_count * HEAD_SIZE * 4
            + 4 * GROUP * row_count * HEAD_SIZE,
        ),
    )(query, keys, values, row_doc, col_doc, attn, grad, lse)


def attach_counts(out_weight, local_counts):
    high = (local_counts // COUNT_BASE).astype(out_weight.dtype)
    low = (local_counts % COUNT_BASE).astype(out_weight.dtype)
    rows = jnp.zeros((16, out_weight.shape[1]), out_weight.dtype)
    rows = rows.at[0, :LANGS].set(high).at[1, :LANGS].set(low)
    return jnp.concatenate([out_weight, rows], axis=0)


def gather_features(block):
    tensor_size = lax.axis_size("tensor")
    me = lax.axis_index("tensor")
    arrived = [(me, block)]
    for shift in range(1, tensor_size):
        pairs = [(index, (index + shift) % tensor_size) for index in range(tensor_size)]
        moved = lax.ppermute(block, "tensor", pairs)
        arrived.append(((me - shift) % tensor_size, moved))
    return arrived


def place_blocks(blocks, rows, width):
    full = jnp.zeros((rows, len(blocks) * width), blocks[0][1].dtype)
    for source, part in blocks:
        full = lax.dynamic_update_slice(full, part, (0, source * width))
    return full


def layer(query, keys, values, out_weight, loss_grad, lengths, languages, labels):
    factor = 1.0 / math.sqrt(HEAD_SIZE)
    row_count = query.shape[0]
    doc_ids = token_docs(lengths[0], row_count).astype(jnp.int32)
    attention_result, log_rows = attention_forward(query, keys, values, doc_ids, factor)
    token_lang = jnp.sum(
        jnp.where(
            doc_ids[:, None] == jnp.arange(DOCS, dtype=jnp.int32)[None, :], languages[0][None, :], 0
        ),
        axis=1,
    )
    counted = labels != -100
    lang_match = token_lang[:, None] == jnp.arange(LANGS, dtype=jnp.int32)[None, :]
    local_counts = jnp.sum((lang_match & counted[:, None]).astype(jnp.int32), axis=0)
    head_rows = out_weight.shape[0] // 2
    gathered = lax.all_gather(
        attach_counts(out_weight[:head_rows], local_counts), "dp", axis=1, tiled=True
    )
    rest = lax.all_gather(out_weight[head_rows:], "dp", axis=1, tiled=True)
    full_weight = jnp.concatenate([gathered[:head_rows], rest], axis=0)
    code = gathered[head_rows : head_rows + 2].astype(jnp.float32)
    code = code.reshape(2, lax.axis_size("dp"), out_weight.shape[1])[:, :, :LANGS]
    counts = jnp.sum(code[0] * COUNT_BASE + code[1], axis=0)
    lang_weight = jnp.sqrt(jnp.sum(counts) / (LANGS * jnp.maximum(counts, 1.0)))
    token_weight = jnp.where(
        counted, jnp.sum(jnp.where(lang_match, lang_weight[None, :], 0.0), axis=1), 0.0
    )
    width = loss_grad.shape[1]
    weighted_blocks = [
        (source, (token_weight[:, None] * part.astype(jnp.float32)).astype(jnp.bfloat16))
        for source, part in gather_features(loss_grad)
    ]
    term_blocks = [
        (
            source,
            lax.dot_general(
                attention_result, part, (((0,), (0,)), ((), ())), preferred_element_type=jnp.float32
            ).astype(jnp.bfloat16),
        )
        for source, part in weighted_blocks
    ]
    local_term = place_blocks(term_blocks, attention_result.shape[1], width)
    projection_part = lax.psum_scatter(local_term, "dp", scatter_dimension=0, tiled=True)
    projection_gradient = lax.all_gather(projection_part, "dp", axis=0, tiled=True)
    weighted = place_blocks(weighted_blocks, loss_grad.shape[0], width)
    local_term, weighted = lax.optimization_barrier((local_term, weighted))
    out_grad = lax.dot_general(
        weighted,
        full_weight,
        (((1,), (1,)), ((), ())),
        preferred_element_type=jnp.float32,
    ).astype(jnp.bfloat16)

    parts = []
    for group in range(keys.shape[1] // HEAD_SIZE):
        parts.append(
            attention_backward_group(
                group, query, keys, values, doc_ids, attention_result, out_grad, log_rows, factor
            )
        )
    query_gradient, key_gradient, value_gradient = (
        jnp.concatenate([part[k] for part in parts], axis=1) for k in range(3)
    )
    return (attention_result, query_gradient, key_gradient, value_gradient, projection_gradient)


def solution(mesh):
    in_specs = (
        P("dp", "tensor"),
        P("dp", "tensor"),
        P("dp", "tensor"),
        P("tensor", "dp"),
        P("dp", "tensor"),
        P("dp", None),
        P("dp", None),
        P("dp"),
    )
    out_specs = (
        P("dp", "tensor"),
        P("dp", "tensor"),
        P("dp", "tensor"),
        P("dp", "tensor"),
        P("tensor", None),
    )
    return jax.shard_map(layer, mesh=mesh, in_specs=in_specs, out_specs=out_specs, check_vma=False)
```

```python
import functools
import math

import jax
import jax.numpy as jnp
from jax import lax
from jax.experimental import pallas as pl
from jax.experimental.pallas import tpu as pltpu
from jax.sharding import PartitionSpec as P


QUERY_HEADS = 40
KEY_VALUE_HEADS = 8
HEAD_SIZE = 128
LANGS = 29
DOCS = 16
COUNT_BASE = 32


def token_docs(length_row, row_count):
    doc_ends = jnp.cumsum(length_row)
    places = jnp.arange(row_count, dtype=jnp.int32)
    return jnp.sum((places[:, None] >= doc_ends[None, :]).astype(jnp.int32), axis=1)


GROUP = QUERY_HEADS // KEY_VALUE_HEADS
ROW_BLOCK = 256
MASKED = -1e30
NT_DIMS = (((1,), (1,)), ((), ()))


def block_mask(row_doc_ref, col_doc_ref, first_row, key_end):
    row_doc = row_doc_ref[first_row : first_row + ROW_BLOCK, :]
    col_doc = col_doc_ref[:, :key_end]
    shape = (ROW_BLOCK, key_end)
    rows = lax.broadcasted_iota(jnp.int32, shape, 0) + first_row
    cols = lax.broadcasted_iota(jnp.int32, shape, 1)
    return (row_doc == col_doc) & (cols <= rows)


def forward_kernel(factor, q_ref, k_ref, v_ref, row_doc_ref, col_doc_ref, o_ref, lse_ref):
    row_count = q_ref.shape[0]
    for block in range(row_count // ROW_BLOCK):
        first_row = block * ROW_BLOCK
        key_end = first_row + ROW_BLOCK
        allowed = block_mask(row_doc_ref, col_doc_ref, first_row, key_end)
        rows = pl.ds(first_row, ROW_BLOCK)

        def head_body(head, carry):
            cols = pl.ds(pl.multiple_of(head * HEAD_SIZE, HEAD_SIZE), HEAD_SIZE)
            query = q_ref[rows, cols]
            scores = lax.dot_general(
                query, k_ref[:key_end, :], NT_DIMS, preferred_element_type=jnp.float32
            ) * factor
            scores = jnp.where(allowed, scores, MASKED)
            top = jnp.max(scores, axis=1, keepdims=True)
            log_total = top + jnp.log(jnp.sum(jnp.exp(scores - top), axis=1, keepdims=True))
            weights = jnp.exp(scores - log_total).astype(jnp.bfloat16)
            result = jnp.dot(weights, v_ref[:key_end, :], preferred_element_type=jnp.float32)
            o_ref[rows, cols] = result.astype(o_ref.dtype)
            lse_ref[0, head, rows, :] = jnp.broadcast_to(log_total, (ROW_BLOCK, HEAD_SIZE))
            return carry

        lax.fori_loop(0, GROUP, head_body, 0)


def backward_kernel(
    factor, q_ref, k_ref, v_ref, row_doc_ref, col_doc_ref, o_ref, do_ref, lse_ref,
    dq_ref, dk_ref, dv_ref, dk_acc, dv_acc,
):
    row_count = q_ref.shape[0]
    dk_acc[...] = jnp.zeros_like(dk_acc)
    dv_acc[...] = jnp.zeros_like(dv_acc)
    for block in range(row_count // ROW_BLOCK):
        first_row = block * ROW_BLOCK
        key_end = first_row + ROW_BLOCK
        allowed = block_mask(row_doc_ref, col_doc_ref, first_row, key_end)
        rows = pl.ds(first_row, ROW_BLOCK)

        def head_body(head, carry):
            cols = pl.ds(pl.multiple_of(head * HEAD_SIZE, HEAD_SIZE), HEAD_SIZE)
            query = q_ref[rows, cols]
            grad = do_ref[rows, cols]
            keys = k_ref[:key_end, :]
            values = v_ref[:key_end, :]
            log_total = lse_ref[0, head, rows, :][:, :1]
            scores = lax.dot_general(query, keys, NT_DIMS, preferred_element_type=jnp.float32) * factor
            scores = jnp.where(allowed, scores, MASKED)
            weights = jnp.exp(scores - log_total)
            dv_acc[:key_end, :] += jnp.dot(
                weights.astype(jnp.bfloat16).T, grad, preferred_element_type=jnp.float32
            )
            weight_grad = lax.dot_general(grad, values, NT_DIMS, preferred_element_type=jnp.float32)
            diagonal = jnp.sum(
                grad.astype(jnp.float32) * o_ref[rows, cols].astype(jnp.float32), axis=1, keepdims=True
            )
            score_grad = (weights * (weight_grad - diagonal) * factor).astype(jnp.bfloat16)
            dq_ref[rows, cols] = jnp.dot(score_grad, keys, preferred_element_type=jnp.float32).astype(
                dq_ref.dtype
            )
            dk_acc[:key_end, :] += jnp.dot(score_grad.T, query, preferred_element_type=jnp.float32)
            return carry

        lax.fori_loop(0, GROUP, head_body, 0)
    dk_ref[...] = dk_acc[...].astype(dk_ref.dtype)
    dv_ref[...] = dv_acc[...].astype(dv_ref.dtype)


def doc_views(doc_ids):
    return doc_ids[:, None], doc_ids[None, :]


def attention_forward(query, keys, values, doc_ids, factor):
    row_count = query.shape[0]
    groups = keys.shape[1] // HEAD_SIZE
    width = GROUP * HEAD_SIZE
    row_doc, col_doc = doc_views(doc_ids)
    flops = 4 * groups * GROUP * row_count * row_count * HEAD_SIZE
    return pl.pallas_call(
        functools.partial(forward_kernel, factor),
        grid=(groups,),
        in_specs=[
            pl.BlockSpec((row_count, width), lambda g: (0, g)),
            pl.BlockSpec((row_count, HEAD_SIZE), lambda g: (0, g)),
            pl.BlockSpec((row_count, HEAD_SIZE), lambda g: (0, g)),
            pl.BlockSpec((row_count, 1), lambda g: (0, 0)),
            pl.BlockSpec((1, row_count), lambda g: (0, 0)),
        ],
        out_specs=[
            pl.BlockSpec((row_count, width), lambda g: (0, g)),
            pl.BlockSpec((1, GROUP, row_count, HEAD_SIZE), lambda g: (g, 0, 0, 0)),
        ],
        out_shape=[
            jax.ShapeDtypeStruct(query.shape, query.dtype),
            jax.ShapeDtypeStruct((groups, GROUP, row_count, HEAD_SIZE), jnp.float32),
        ],
        compiler_params=pltpu.CompilerParams(vmem_limit_bytes=48 * 1024 * 1024),
        cost_estimate=pl.CostEstimate(
            flops=flops // 2, transcendentals=groups * GROUP * row_count * row_count // 2,
            bytes_accessed=4 * query.size + 8 * keys.size + 8 * groups * GROUP * row_count * HEAD_SIZE,
        ),
    )(query, keys, values, row_doc, col_doc)


def attention_backward_group(group, query, keys, values, doc_ids, attn, grad, lse, factor):
    row_count = query.shape[0]
    width = GROUP * HEAD_SIZE
    row_doc, col_doc = doc_views(doc_ids)
    flops = 10 * GROUP * row_count * row_count * HEAD_SIZE
    return pl.pallas_call(
        functools.partial(backward_kernel, factor),
        grid=(1,),
        in_specs=[
            pl.BlockSpec((row_count, width), lambda g: (0, group)),
            pl.BlockSpec((row_count, HEAD_SIZE), lambda g: (0, group)),
            pl.BlockSpec((row_count, HEAD_SIZE), lambda g: (0, group)),
            pl.BlockSpec((row_count, 1), lambda g: (0, 0)),
            pl.BlockSpec((1, row_count), lambda g: (0, 0)),
            pl.BlockSpec((row_count, width), lambda g: (0, group)),
            pl.BlockSpec((row_count, width), lambda g: (0, group)),
            pl.BlockSpec((1, GROUP, row_count, HEAD_SIZE), lambda g: (group, 0, 0, 0)),
        ],
        out_specs=[
            pl.BlockSpec((row_count, width), lambda g: (0, 0)),
            pl.BlockSpec((row_count, HEAD_SIZE), lambda g: (0, 0)),
            pl.BlockSpec((row_count, HEAD_SIZE), lambda g: (0, 0)),
        ],
        out_shape=[
            jax.ShapeDtypeStruct((row_count, width), query.dtype),
            jax.ShapeDtypeStruct((row_count, HEAD_SIZE), keys.dtype),
            jax.ShapeDtypeStruct((row_count, HEAD_SIZE), keys.dtype),
        ],
        scratch_shapes=[
            pltpu.VMEM((row_count, HEAD_SIZE), jnp.float32),
            pltpu.VMEM((row_count, HEAD_SIZE), jnp.float32),
        ],
        compiler_params=pltpu.CompilerParams(vmem_limit_bytes=48 * 1024 * 1024),
        cost_estimate=pl.CostEstimate(
            flops=flops // 2, transcendentals=GROUP * row_count * row_count // 2,
            bytes_accessed=2 * 4 * row_count * width + 4 * row_count * HEAD_SIZE * 4
            + 4 * GROUP * row_count * HEAD_SIZE,
        ),
    )(query, keys, values, row_doc, col_doc, attn, grad, lse)


def attach_counts(out_weight, local_counts):
    high = (local_counts // COUNT_BASE).astype(out_weight.dtype)
    low = (local_counts % COUNT_BASE).astype(out_weight.dtype)
    rows = jnp.zeros((16, out_weight.shape[1]), out_weight.dtype)
    rows = rows.at[0, :LANGS].set(high).at[1, :LANGS].set(low)
    return jnp.concatenate([out_weight, rows], axis=0)


def gather_features(block):
    tensor_size = lax.axis_size("tensor")
    me = lax.axis_index("tensor")
    arrived = [(me, block)]
    for shift in range(1, tensor_size):
        pairs = [(index, (index + shift) % tensor_size) for index in range(tensor_size)]
        moved = lax.ppermute(block, "tensor", pairs)
        arrived.append(((me - shift) % tensor_size, moved))
    return arrived


def place_blocks(blocks, rows, width):
    full = jnp.zeros((rows, len(blocks) * width), blocks[0][1].dtype)
    for source, part in blocks:
        full = lax.dynamic_update_slice(full, part, (0, source * width))
    return full


def layer(query, keys, values, out_weight, loss_grad, lengths, languages, labels):
    factor = 1.0 / math.sqrt(HEAD_SIZE)
    row_count = query.shape[0]
    doc_ids = token_docs(lengths[0], row_count).astype(jnp.int32)
    attention_result, log_rows = attention_forward(query, keys, values, doc_ids, factor)
    token_lang = jnp.sum(
        jnp.where(
            doc_ids[:, None] == jnp.arange(DOCS, dtype=jnp.int32)[None, :], languages[0][None, :], 0
        ),
        axis=1,
    )
    counted = labels != -100
    lang_match = token_lang[:, None] == jnp.arange(LANGS, dtype=jnp.int32)[None, :]
    local_counts = jnp.sum((lang_match & counted[:, None]).astype(jnp.int32), axis=0)
    weight_rows = out_weight.shape[0]
    gathered = lax.all_gather(
        attach_counts(out_weight, local_counts), "dp", axis=1, tiled=True
    )
    full_weight = gathered[:weight_rows]
    code = gathered[weight_rows : weight_rows + 2].astype(jnp.float32)
    code = code.reshape(2, lax.axis_size("dp"), out_weight.shape[1])[:, :, :LANGS]
    counts = jnp.sum(code[0] * COUNT_BASE + code[1], axis=0)
    lang_weight = jnp.sqrt(jnp.sum(counts) / (LANGS * jnp.maximum(counts, 1.0)))
    token_weight = jnp.where(
        counted, jnp.sum(jnp.where(lang_match, lang_weight[None, :], 0.0), axis=1), 0.0
    )
    width = loss_grad.shape[1]
    weighted_blocks = [
        (source, (token_weight[:, None] * part.astype(jnp.float32)).astype(jnp.bfloat16))
        for source, part in gather_features(loss_grad)
    ]
    term_blocks = [
        (
            source,
            lax.dot_general(
                attention_result, part, (((0,), (0,)), ((), ())), preferred_element_type=jnp.float32
            ).astype(jnp.bfloat16),
        )
        for source, part in weighted_blocks
    ]
    local_term = place_blocks(term_blocks, attention_result.shape[1], width)
    projection_part = lax.psum_scatter(local_term, "dp", scatter_dimension=0, tiled=True)
    projection_gradient = lax.all_gather(projection_part, "dp", axis=0, tiled=True)
    weighted = place_blocks(weighted_blocks, loss_grad.shape[0], width)
    local_term, weighted = lax.optimization_barrier((local_term, weighted))
    out_grad = lax.dot_general(
        weighted,
        full_weight,
        (((1,), (1,)), ((), ())),
        preferred_element_type=jnp.float32,
    ).astype(jnp.bfloat16)

    parts = []
    for group in range(keys.shape[1] // HEAD_SIZE):
        parts.append(
            attention_backward_group(
                group, query, keys, values, doc_ids, attention_result, out_grad, log_rows, factor
            )
        )
    query_gradient, key_gradient, value_gradient = (
        jnp.concatenate([part[k] for part in parts], axis=1) for k in range(3)
    )
    return (attention_result, query_gradient, key_gradient, value_gradient, projection_gradient)


def solution(mesh):
    in_specs = (
        P("dp", "tensor"),
        P("dp", "tensor"),
        P("dp", "tensor"),
        P("tensor", "dp"),
        P("dp", "tensor"),
        P("dp", None),
        P("dp", None),
        P("dp"),
    )
    out_specs = (
        P("dp", "tensor"),
        P("dp", "tensor"),
        P("dp", "tensor"),
        P("dp", "tensor"),
        P("tensor", None),
    )
    return jax.shard_map(layer, mesh=mesh, in_specs=in_specs, out_specs=out_specs, check_vma=False)
```
